512 devices in a mesh: section: 2 (over core), expert: 32 (over z_lo, x), tensor: 8 (over y, z_hi).
Axes of the slice: x: 4, y: 4, z: 16 (z_hi: 2, z_lo: 8; z = z_hi * 8 + z_lo), core: 2. Of those that a mesh axis runs over, the one named last changes fastest.
Arguments:
- sent: bfloat16 [2, 4096, 4096], P('section', ('expert', 'tensor')), may hold values from -20 to 20
- norm_gain: float32 [2, 4096], P('section'), may hold values from 0.1 to 1.9
- router: bfloat16 [2, 4096, 32], P('section'), may hold values from -0.09375 to 0.09375
- w_in: bfloat16 [2, 32, 4096, 2048], P('section', 'expert', None, 'tensor'), may hold values from -0.09375 to 0.09375
- w_out: bfloat16 [2, 32, 2048, 4096], P('section', 'expert', 'tensor'), may hold values from -0.125 to 0.125
- expert_ids: int32 [2, 4096, 2], P('section', ('expert', 'tensor')), may hold values from 0 to 31, as said below
Outputs:
- handed: bfloat16 [2, 4096, 4096], P('section', ('expert', 'tensor'))
The draws below stay inside these ranges and needn't reach their ends.
Inputs may be any that keep to these rules, and one draw needn't show every extreme that they name: `expert_ids`: each token names two different experts of the 32.
All inputs are finite; a program needn't handle non-finite values.
Results may differ from the reference program's by a relative error of at most 0.0054.
Values may be sent and summed in bfloat16 or wider, within the bound.
No kernel may reach another device: no remote copies, remote signals or barrier semaphores. Data moves between devices by JAX's collectives and lax.ppermute only.
A program may use at most 64 MiB of HBM per device.

```python
import jax
import jax.numpy as jnp
from jax import lax

D = 4096
FF = 2048
TOK_DEV = 16
EXPERTS = 32
CAP = 2
TOKENS = 4096
N_SECTION = 2
N_TENSOR = 8


def draw_sent(key, part):
    subkeys = jax.random.split(key, 3)
    values = jnp.clip(jax.random.normal(subkeys[0], (N_SECTION, TOKENS, D), jnp.float32), -4.0, 4.0)
    row_scale = jnp.exp(jax.random.uniform(subkeys[1], (N_SECTION, TOKENS, 1), jnp.float32, -0.8, 0.8))
    col_scale = jnp.exp(jax.random.uniform(subkeys[2], (N_SECTION, 1, D), jnp.float32, -0.8, 0.8))
    return (values * row_scale * col_scale).astype(jnp.bfloat16)


def draw_expert_ids(key, part):
    subkeys = jax.random.split(key, 5)
    grid_shape = (N_SECTION, TOKENS)
    lowest = jnp.minimum(jax.random.randint(subkeys[0], grid_shape, 0, EXPERTS), jax.random.randint(subkeys[1], grid_shape, 0, EXPERTS))
    lowest = jnp.minimum(lowest, jax.random.randint(subkeys[2], grid_shape, 0, EXPERTS))
    relabel = jax.random.permutation(subkeys[3], EXPERTS).astype(jnp.int32)
    first_pick = relabel[lowest]
    offset = jax.random.randint(subkeys[4], grid_shape, 1, EXPERTS)
    second_pick = (first_pick + offset) % EXPERTS
    return jnp.stack([first_pick, second_pick], axis=-1).astype(jnp.int32)


def levels(rng, dims, cuts, low, largest):
    factor_of = 1.0
    for dim, parts in cuts:
        steps = jax.random.uniform(jax.random.fold_in(jax.random.fold_in(rng, 6), dim), (parts,), jnp.float32, low / len(cuts), largest / len(cuts))
        factor_of = factor_of * jnp.repeat(jnp.exp(steps), dims[dim] // parts).reshape((-1,) + (1,) * (len(dims) - 1 - dim))
    return factor_of


def bell_draw(key, extent, deviation, most, shards=(), held_as=jnp.bfloat16):
    gain = levels(key, extent, shards, -0.22, 0.18) if shards else 1.0
    values = jax.random.normal(key, extent, jnp.float32) * deviation * gain
    return jnp.minimum(jnp.maximum(values, -most), most).astype(held_as)


def setup_inputs(seed: int = 0) -> dict:
    arg_keys = jax.random.split(jax.random.key(seed), 7)
    return {
        "sent": draw_sent(jax.random.fold_in(arg_keys[6], 71), 0),
        "norm_gain": jnp.clip(1.0 + 0.18 * jax.random.normal(arg_keys[1], (N_SECTION, D), jnp.float32), 0.1, 1.9),
        "router": bell_draw(arg_keys[2], (N_SECTION, D, EXPERTS), D ** -0.5, 0.09375, ((0, 2),)),
        "w_in": bell_draw(arg_keys[3], (N_SECTION, EXPERTS, D, FF), D ** -0.5, 0.09375, ((0, 2), (1, 32), (3, 8))),
        "w_out": bell_draw(arg_keys[4], (N_SECTION, EXPERTS, FF, D), FF ** -0.5, 0.125, ((0, 2), (1, 32), (2, 8))),
        "expert_ids": draw_expert_ids(jax.random.fold_in(arg_keys[6], 71), 0),
    }


def normalize(inputs, gain_row):
    widened = inputs.astype(jnp.float32)
    mean_sq = lax.optimization_barrier(jnp.mean(widened * widened, axis=-1, keepdims=True))
    return (widened * lax.rsqrt(mean_sq + 1e-05) * gain_row).astype(jnp.bfloat16)

def route(normed, router_mat, expert_pick, tok_block, capacity):
    logits = jnp.dot(normed, router_mat, preferred_element_type=jnp.float32)
    experts = router_mat.shape[1]
    labels = jnp.arange(experts, dtype=jnp.int32)
    pair_hot = (expert_pick[:, :, None] == labels[None, None, :]).astype(jnp.float32)
    picked = lax.optimization_barrier(jnp.sum(pair_hot * logits[:, None, :], axis=-1))
    squashed = jax.nn.sigmoid(picked)
    gate_vals = squashed / lax.optimization_barrier(jnp.sum(squashed, axis=-1, keepdims=True))
    blocks = expert_pick.shape[0] // tok_block
    pair_order = jnp.transpose(expert_pick.reshape(blocks, tok_block, 2), (0, 2, 1)).reshape(blocks, 2 * tok_block)
    one_hot = (pair_order[:, :, None] == labels[None, None, :]).astype(jnp.int32)
    before = (jnp.cumsum(one_hot, axis=1) - one_hot).astype(jnp.int32)
    pair_ranks = lax.optimization_barrier(jnp.sum(before * one_hot, axis=-1)).astype(jnp.int32)
    pair_ranks = jnp.transpose(pair_ranks.reshape(blocks, 2, tok_block), (0, 2, 1)).reshape(-1, 2)
    is_kept = pair_ranks < capacity
    return (gate_vals, pair_ranks, is_kept)

def layer(inputs, gain_row, router_mat, w_first, w_second, expert_pick):
    normed = normalize(inputs, gain_row)
    gate_vals, pair_ranks, is_kept = route(normed, router_mat, expert_pick, TOK_DEV, CAP)
    tok_total = inputs.shape[0]
    blocks = tok_total // TOK_DEV
    block_of = (jnp.arange(tok_total, dtype=jnp.int32) // TOK_DEV)[:, None]
    flat_slot = (expert_pick * (blocks * CAP) + block_of * CAP + pair_ranks).astype(jnp.int32)
    slot_total = EXPERTS * blocks * CAP
    target = jnp.where(is_kept, flat_slot, slot_total).reshape(-1)
    source_tok = jnp.broadcast_to(jnp.arange(tok_total, dtype=jnp.int32)[:, None], (tok_total, 2)).reshape(-1)
    owner_row = jnp.full((slot_total,), tok_total, jnp.int32).at[target].set(source_tok, mode='drop')
    padded = jnp.concatenate([normed, jnp.zeros((1, D), jnp.bfloat16)], axis=0)
    slot_rows = padded[owner_row].reshape(EXPERTS, blocks * CAP, D)
    group_width = FF // N_TENSOR

    def expert_ffn(operands):
        rows_in, first_mat, second_mat = operands
        hidden = jax.nn.gelu(jnp.dot(rows_in, first_mat, preferred_element_type=jnp.float32)).astype(jnp.bfloat16)
        summed = jnp.zeros((rows_in.shape[0], D), jnp.float32)
        for group_idx in range(N_TENSOR):
            lower = group_idx * group_width
            partial_value = jnp.dot(hidden[:, lower:lower + group_width], second_mat[lower:lower + group_width], preferred_element_type=jnp.float32).astype(jnp.bfloat16)
            summed = summed + partial_value.astype(jnp.float32)
        return summed.astype(jnp.bfloat16)
    expert_out = lax.map(expert_ffn, (slot_rows, w_first, w_second)).reshape(slot_total, D)
    picked = expert_out[jnp.where(is_kept, flat_slot, 0)].astype(jnp.float32)
    pair_weight = jnp.where(is_kept, gate_vals, 0.0)
    return (inputs.astype(jnp.float32) + lax.optimization_barrier(jnp.sum(pair_weight[:, :, None] * picked, axis=1))).astype(jnp.bfloat16)

def reference(sent, norm_gain, router, w_in, w_out, expert_ids):
    layer_outs = []
    for section_idx in range(N_SECTION):
        prior = (section_idx - 1) % N_SECTION
        layer_outs.append(layer(sent[prior], norm_gain[section_idx], router[section_idx], w_in[section_idx], w_out[section_idx], expert_ids[section_idx]))
    handed = [layer_outs[(section_idx - 1) % N_SECTION] for section_idx in range(N_SECTION)]
    return jnp.stack(handed)
```

```python
import jax
import jax.numpy as jnp
from jax import lax
from jax.sharding import Mesh
from jax.sharding import PartitionSpec as P


def passed_along(value, axis, steps):
    count = lax.axis_size(axis)
    pairs = [(source, (source + steps) % count) for source in range(count)]
    return lax.ppermute(value, axis, pairs)


def normalize(inputs, gain_row):
    widened = inputs.astype(jnp.float32)
    mean_sq = jnp.mean(widened * widened, axis=-1, keepdims=True)
    return (widened * lax.rsqrt(mean_sq + 1e-05) * gain_row).astype(jnp.bfloat16)


def route(normed, router_mat, expert_pick, tok_block, capacity):
    logits = jnp.dot(normed, router_mat, preferred_element_type=jnp.float32)
    experts = router_mat.shape[1]
    labels = jnp.arange(experts, dtype=jnp.int32)
    pair_hot = (expert_pick[:, :, None] == labels[None, None, :]).astype(jnp.float32)
    picked = jnp.sum(pair_hot * logits[:, None, :], axis=-1)
    squashed = jax.nn.sigmoid(picked)
    gate_vals = squashed / jnp.sum(squashed, axis=-1, keepdims=True)
    blocks = expert_pick.shape[0] // tok_block
    pair_order = jnp.transpose(expert_pick.reshape(blocks, tok_block, 2), (0, 2, 1)).reshape(
        blocks, 2 * tok_block
    )
    one_hot = (pair_order[:, :, None] == labels[None, None, :]).astype(jnp.int32)
    before = jnp.cumsum(one_hot, axis=1) - one_hot
    pair_ranks = jnp.sum(before * one_hot, axis=-1)
    pair_ranks = jnp.transpose(pair_ranks.reshape(blocks, 2, tok_block), (0, 2, 1)).reshape(-1, 2)
    is_kept = pair_ranks < capacity
    return (gate_vals, pair_ranks, is_kept)


def on_device(sent, norm_gain, router, w_in, w_out, expert_ids):
    arrived = passed_along(sent, "section", 1)[0]
    tok_count = arrived.shape[0]
    model_width = arrived.shape[1]
    experts = router.shape[2]
    top_count = expert_ids.shape[2]
    n_y = lax.axis_size("y")
    capacity = max(2, (5 * top_count * tok_count + 4 * experts - 1) // (4 * experts))
    normed = normalize(arrived, norm_gain[0])
    own_pick = expert_ids[0]
    partner_rows = passed_along(normed, "zh", 1)
    partner_pick = passed_along(own_pick, "zh", 1)
    rows_both = jnp.concatenate([normed, partner_rows], axis=0)
    pick_both = jnp.concatenate([own_pick, partner_pick], axis=0)
    gate_vals, pair_ranks, is_kept = route(rows_both, router[0], pick_both, tok_count, capacity)
    n_tok = 2 * tok_count
    block_of = (jnp.arange(n_tok, dtype=jnp.int32) // tok_count)[:, None]
    per_expert = 2 * capacity
    slot_ids = pick_both * per_expert + block_of * capacity + pair_ranks
    slot_count = experts * per_expert
    slot_labels = jnp.arange(slot_count, dtype=jnp.int32)
    slot_hot = ((slot_ids[:, :, None] == slot_labels[None, None, :]) & is_kept[:, :, None]).astype(
        jnp.float32
    )
    placement = jnp.transpose(jnp.sum(slot_hot, axis=1)).astype(jnp.bfloat16)
    combine_mat = jnp.sum(slot_hot * gate_vals[:, :, None], axis=1)
    send_rows = jnp.dot(placement, rows_both, preferred_element_type=jnp.float32).astype(jnp.bfloat16)
    slot_grid = send_rows.reshape(experts, per_expert, model_width)
    received = lax.all_to_all(slot_grid, "expert", split_axis=0, concat_axis=0, tiled=True)
    gathered = lax.all_gather(received[None], "y", axis=0, tiled=True)
    rows_in = gathered.reshape(-1, model_width)
    hidden = jax.nn.gelu(
        jnp.dot(rows_in, w_in[0, 0], preferred_element_type=jnp.float32)
    ).astype(jnp.bfloat16)
    partial = jnp.dot(hidden, w_out[0, 0], preferred_element_type=jnp.float32).astype(jnp.bfloat16)
    summed = lax.psum_scatter(
        partial.reshape(n_y, -1, model_width), "y", scatter_dimension=0, tiled=True
    )
    back = lax.all_to_all(
        summed.reshape(experts, per_expert, model_width), "expert", split_axis=0, concat_axis=0, tiled=True
    )
    half_sum = jnp.dot(
        combine_mat,
        back.reshape(slot_count, model_width).astype(jnp.float32),
        precision=lax.Precision.HIGHEST,
    )
    from_partner = passed_along(half_sum[tok_count:].astype(jnp.bfloat16), "zh", 1)
    combined = arrived.astype(jnp.float32) + half_sum[:tok_count] + from_partner.astype(jnp.float32)
    return passed_along(combined.astype(jnp.bfloat16)[None], "section", 1)


def solution(mesh):
    sizes = dict(mesh.shape)
    n_tensor = sizes["tensor"]
    fine = Mesh(
        mesh.devices.reshape(sizes["section"], sizes["expert"], n_tensor // 2, 2),
        ("section", "expert", "y", "zh"),
    )
    tokens = ("expert", "y", "zh")
    hidden_units = ("y", "zh")
    return jax.shard_map(
        on_device,
        mesh=fine,
        in_specs=(
            P("section", tokens, None),
            P("section", None),
            P("section", None, None),
            P("section", "expert", None, hidden_units),
            P("section", "expert", hidden_units, None),
            P("section", tokens, None),
        ),
        out_specs=P("section", tokens, None),
        check_vma=False,
    )
```

```python
import jax
import jax.numpy as jnp
from jax import lax
from jax.sharding import Mesh
from jax.sharding import PartitionSpec as P


def passed_along(value, axis, steps):
    count = lax.axis_size(axis)
    pairs = [(source, (source + steps) % count) for source in range(count)]
    return lax.ppermute(value, axis, pairs)


def normalize(inputs, gain_row):
    widened = inputs.astype(jnp.float32)
    mean_sq = jnp.mean(widened * widened, axis=-1, keepdims=True)
    return (widened * lax.rsqrt(mean_sq + 1e-05) * gain_row).astype(jnp.bfloat16)


def route(normed, router_mat, expert_pick, tok_block, capacity):
    logits = jnp.dot(normed, router_mat, preferred_element_type=jnp.float32)
    experts = router_mat.shape[1]
    labels = jnp.arange(experts, dtype=jnp.int32)
    pair_hot = (expert_pick[:, :, None] == labels[None, None, :]).astype(jnp.float32)
    picked = jnp.sum(pair_hot * logits[:, None, :], axis=-1)
    squashed = jax.nn.sigmoid(picked)
    gate_vals = squashed / jnp.sum(squashed, axis=-1, keepdims=True)
    blocks = expert_pick.shape[0] // tok_block
    pair_order = jnp.transpose(expert_pick.reshape(blocks, tok_block, 2), (0, 2, 1)).reshape(
        blocks, 2 * tok_block
    )
    one_hot = (pair_order[:, :, None] == labels[None, None, :]).astype(jnp.int32)
    before = jnp.cumsum(one_hot, axis=1) - one_hot
    pair_ranks = jnp.sum(before * one_hot, axis=-1)
    pair_ranks = jnp.transpose(pair_ranks.reshape(blocks, 2, tok_block), (0, 2, 1)).reshape(-1, 2)
    is_kept = pair_ranks < capacity
    return (gate_vals, pair_ranks, is_kept)


def dispatch(rows, pick, router_mat, capacity):
    tok_count, model_width = rows.shape
    experts = router_mat.shape[1]
    gate_vals, pair_ranks, is_kept = route(rows, router_mat, pick, tok_count, capacity)
    slot_ids = pick * capacity + pair_ranks
    slot_count = experts * capacity
    slot_labels = jnp.arange(slot_count, dtype=jnp.int32)
    slot_hot = ((slot_ids[:, :, None] == slot_labels[None, None, :]) & is_kept[:, :, None]).astype(
        jnp.float32
    )
    placement = jnp.transpose(jnp.sum(slot_hot, axis=1)).astype(jnp.bfloat16)
    combine_mat = jnp.sum(slot_hot * gate_vals[:, :, None], axis=1)
    send_rows = jnp.dot(placement, rows, preferred_element_type=jnp.float32).astype(jnp.bfloat16)
    return send_rows.reshape(experts, capacity, model_width), combine_mat


def expert_pass(slot_grid, combine_mat, w_first, w_second):
    experts, capacity, model_width = slot_grid.shape
    n_y = lax.axis_size("y")
    received = lax.all_to_all(slot_grid, "expert", split_axis=0, concat_axis=0, tiled=True)
    gathered = lax.all_gather(received[None], "y", axis=0, tiled=True)
    rows_in = gathered.reshape(-1, model_width)
    hidden = jax.nn.gelu(
        jnp.dot(rows_in, w_first, preferred_element_type=jnp.float32)
    ).astype(jnp.bfloat16)
    partial = jnp.dot(hidden, w_second, preferred_element_type=jnp.float32).astype(jnp.bfloat16)
    summed = lax.psum_scatter(
        partial.reshape(n_y, -1, model_width), "y", scatter_dimension=0, tiled=True
    )
    back = lax.all_to_all(
        summed.reshape(experts, capacity, model_width), "expert", split_axis=0, concat_axis=0, tiled=True
    )
    return jnp.dot(
        combine_mat,
        back.reshape(experts * capacity, model_width).astype(jnp.float32),
        precision=lax.Precision.HIGHEST,
    )


def on_device(sent, norm_gain, router, w_in, w_out, expert_ids):
    arrived = passed_along(sent, "section", 1)[0]
    tok_count = arrived.shape[0]
    experts = router.shape[2]
    top_count = expert_ids.shape[2]
    capacity = max(2, (5 * top_count * tok_count + 4 * experts - 1) // (4 * experts))
    normed = normalize(arrived, norm_gain[0])
    own_pick = expert_ids[0]
    partner_rows = passed_along(normed, "zh", 1)
    partner_pick = passed_along(own_pick, "zh", 1)
    w_first = w_in[0, 0]
    w_second = w_out[0, 0]
    own_slots, own_combine = dispatch(normed, own_pick, router[0], capacity)
    own_half = expert_pass(own_slots, own_combine, w_first, w_second)
    partner_slots, partner_combine = dispatch(partner_rows, partner_pick, router[0], capacity)
    partner_half = expert_pass(partner_slots, partner_combine, w_first, w_second)
    from_partner = passed_along(partner_half.astype(jnp.bfloat16), "zh", 1)
    combined = arrived.astype(jnp.float32) + own_half + from_partner.astype(jnp.float32)
    return passed_along(combined.astype(jnp.bfloat16)[None], "section", 1)


def solution(mesh):
    sizes = dict(mesh.shape)
    n_tensor = sizes["tensor"]
    fine = Mesh(
        mesh.devices.reshape(sizes["section"], sizes["expert"], n_tensor // 2, 2),
        ("section", "expert", "y", "zh"),
    )
    tokens = ("expert", "y", "zh")
    hidden_units = ("y", "zh")
    return jax.shard_map(
        on_device,
        mesh=fine,
        in_specs=(
            P("section", tokens, None),
            P("section", None),
            P("section", None, None),
            P("section", "expert", None, hidden_units),
            P("section", "expert", hidden_units, None),
            P("section", tokens, None),
        ),
        out_specs=P("section", tokens, None),
        check_vma=False,
    )
```

```python
import jax
import jax.numpy as jnp
from jax import lax
from jax.sharding import Mesh
from jax.sharding import PartitionSpec as P


def passed_along(value, axis, steps):
    count = lax.axis_size(axis)
    pairs = [(source, (source + steps) % count) for source in range(count)]
    return lax.ppermute(value, axis, pairs)


def normalize(inputs, gain_row):
    widened = inputs.astype(jnp.float32)
    mean_sq = jnp.mean(widened * widened, axis=-1, keepdims=True)
    return (widened * lax.rsqrt(mean_sq + 1e-05) * gain_row).astype(jnp.bfloat16)


def route(normed, router_mat, expert_pick, tok_block, capacity):
    logits = jnp.dot(normed, router_mat, preferred_element_type=jnp.float32)
    experts = router_mat.shape[1]
    labels = jnp.arange(experts, dtype=jnp.int32)
    pair_hot = (expert_pick[:, :, None] == labels[None, None, :]).astype(jnp.float32)
    picked = jnp.sum(pair_hot * logits[:, None, :], axis=-1)
    squashed = jax.nn.sigmoid(picked)
    gate_vals = squashed / jnp.sum(squashed, axis=-1, keepdims=True)
    blocks = expert_pick.shape[0] // tok_block
    pair_order = jnp.transpose(expert_pick.reshape(blocks, tok_block, 2), (0, 2, 1)).reshape(
        blocks, 2 * tok_block
    )
    one_hot = (pair_order[:, :, None] == labels[None, None, :]).astype(jnp.int32)
    before = jnp.cumsum(one_hot, axis=1) - one_hot
    pair_ranks = jnp.sum(before * one_hot, axis=-1)
    pair_ranks = jnp.transpose(pair_ranks.reshape(blocks, 2, tok_block), (0, 2, 1)).reshape(-1, 2)
    is_kept = pair_ranks < capacity
    return (gate_vals, pair_ranks, is_kept)


def dispatch(rows, pick, router_mat, capacity):
    tok_count, model_width = rows.shape
    experts = router_mat.shape[1]
    gate_vals, pair_ranks, is_kept = route(rows, router_mat, pick, tok_count, capacity)
    slot_ids = pick * capacity + pair_ranks
    slot_count = experts * capacity
    slot_labels = jnp.arange(slot_count, dtype=jnp.int32)
    slot_hot = ((slot_ids[:, :, None] == slot_labels[None, None, :]) & is_kept[:, :, None]).astype(
        jnp.float32
    )
    placement = jnp.transpose(jnp.sum(slot_hot, axis=1)).astype(jnp.bfloat16)
    combine_mat = jnp.sum(slot_hot * gate_vals[:, :, None], axis=1)
    send_rows = jnp.dot(placement, rows, preferred_element_type=jnp.float32).astype(jnp.bfloat16)
    return send_rows.reshape(experts, capacity, model_width), combine_mat


def expert_pass(slot_grid, combine_mat, w_first, w_second):
    experts, capacity, model_width = slot_grid.shape
    n_y = lax.axis_size("y")
    received = lax.all_to_all(slot_grid, "expert", split_axis=0, concat_axis=0, tiled=True)
    shifted = [received] + [passed_along(received, "y", k) for k in range(1, n_y)]
    rows_in = jnp.concatenate(shifted, axis=0).reshape(-1, model_width)
    hidden = jax.nn.gelu(
        jnp.dot(rows_in, w_first, preferred_element_type=jnp.float32)
    ).astype(jnp.bfloat16)
    partial = jnp.dot(hidden, w_second, preferred_element_type=jnp.float32).astype(jnp.bfloat16)
    partial = partial.reshape(n_y, experts * capacity, model_width)
    summed = partial[0].astype(jnp.float32)
    for k in range(1, n_y):
        summed = summed + passed_along(partial[k], "y", n_y - k).astype(jnp.float32)
    back = lax.all_to_all(
        summed.astype(jnp.bfloat16).reshape(experts, capacity, model_width),
        "expert", split_axis=0, concat_axis=0, tiled=True,
    )
    return jnp.dot(
        combine_mat,
        back.reshape(experts * capacity, model_width).astype(jnp.float32),
        precision=lax.Precision.HIGHEST,
    )


def on_device(sent, norm_gain, router, w_in, w_out, expert_ids):
    arrived = passed_along(sent, "section", 1)[0]
    tok_count = arrived.shape[0]
    experts = router.shape[2]
    top_count = expert_ids.shape[2]
    capacity = max(2, (5 * top_count * tok_count + 4 * experts - 1) // (4 * experts))
    normed = normalize(arrived, norm_gain[0])
    own_pick = expert_ids[0]
    partner_rows = passed_along(normed, "zh", 1)
    partner_pick = passed_along(own_pick, "zh", 1)
    w_first = w_in[0, 0]
    w_second = w_out[0, 0]
    own_slots, own_combine = dispatch(normed, own_pick, router[0], capacity)
    own_half = expert_pass(own_slots, own_combine, w_first, w_second)
    partner_slots, partner_combine = dispatch(partner_rows, partner_pick, router[0], capacity)
    partner_half = expert_pass(partner_slots, partner_combine, w_first, w_second)
    from_partner = passed_along(partner_half.astype(jnp.bfloat16), "zh", 1)
    combined = arrived.astype(jnp.float32) + own_half + from_partner.astype(jnp.float32)
    return passed_along(combined.astype(jnp.bfloat16)[None], "section", 1)


def solution(mesh):
    sizes = dict(mesh.shape)
    n_tensor = sizes["tensor"]
    fine = Mesh(
        mesh.devices.reshape(sizes["section"], sizes["expert"], n_tensor // 2, 2),
        ("section", "expert", "y", "zh"),
    )
    tokens = ("expert", "y", "zh")
    hidden_units = ("y", "zh")
    return jax.shard_map(
        on_device,
        mesh=fine,
        in_specs=(
            P("section", tokens, None),
            P("section", None),
            P("section", None, None),
            P("section", "expert", None, hidden_units),
            P("section", "expert", hidden_units, None),
            P("section", tokens, None),
        ),
        out_specs=P("section", tokens, None),
        check_vma=False,
    )
```

```python
import jax
import jax.numpy as jnp
from jax import lax
from jax.sharding import Mesh
from jax.sharding import PartitionSpec as P


def passed_along(value, axis, steps):
    count = lax.axis_size(axis)
    pairs = [(source, (source + steps) % count) for source in range(count)]
    return lax.ppermute(value, axis, pairs)


def normalize(inputs, gain_row):
    widened = inputs.astype(jnp.float32)
    mean_sq = jnp.mean(widened * widened, axis=-1, keepdims=True)
    return (widened * lax.rsqrt(mean_sq + 1e-05) * gain_row).astype(jnp.bfloat16)


def route(normed, router_mat, expert_pick, tok_block, capacity):
    logits = jnp.dot(normed, router_mat, preferred_element_type=jnp.float32)
    experts = router_mat.shape[1]
    labels = jnp.arange(experts, dtype=jnp.int32)
    pair_hot = (expert_pick[:, :, None] == labels[None, None, :]).astype(jnp.float32)
    picked = jnp.sum(pair_hot * logits[:, None, :], axis=-1)
    squashed = jax.nn.sigmoid(picked)
    gate_vals = squashed / jnp.sum(squashed, axis=-1, keepdims=True)
    blocks = expert_pick.shape[0] // tok_block
    pair_order = jnp.transpose(expert_pick.reshape(blocks, tok_block, 2), (0, 2, 1)).reshape(
        blocks, 2 * tok_block
    )
    one_hot = (pair_order[:, :, None] == labels[None, None, :]).astype(jnp.int32)
    before = jnp.cumsum(one_hot, axis=1) - one_hot
    pair_ranks = jnp.sum(before * one_hot, axis=-1)
    pair_ranks = jnp.transpose(pair_ranks.reshape(blocks, 2, tok_block), (0, 2, 1)).reshape(-1, 2)
    is_kept = pair_ranks < capacity
    return (gate_vals, pair_ranks, is_kept)


def dispatch(rows, pick, router_mat, capacity):
    tok_count, model_width = rows.shape
    experts = router_mat.shape[1]
    gate_vals, pair_ranks, is_kept = route(rows, router_mat, pick, tok_count, capacity)
    slot_ids = pair_ranks * experts + pick
    slot_count = experts * capacity
    slot_labels = jnp.arange(slot_count, dtype=jnp.int32)
    slot_hot = ((slot_ids[:, :, None] == slot_labels[None, None, :]) & is_kept[:, :, None]).astype(
        jnp.float32
    )
    placement = jnp.transpose(jnp.sum(slot_hot, axis=1)).astype(jnp.bfloat16)
    combine_mat = jnp.sum(slot_hot * gate_vals[:, :, None], axis=1)
    send_rows = jnp.dot(placement, rows, preferred_element_type=jnp.float32).astype(jnp.bfloat16)
    return send_rows.reshape(capacity, experts, model_width), combine_mat


def expert_pass(slot_grid, combine_mat, w_first, w_second):
    capacity, experts, model_width = slot_grid.shape
    n_y = lax.axis_size("y")
    received = lax.all_to_all(slot_grid, "expert", split_axis=1, concat_axis=1, tiled=True)
    summed = None
    for k in range(n_y):
        rows_in = received if k == 0 else passed_along(received, "y", k)
        hidden = jax.nn.gelu(
            jnp.dot(rows_in.reshape(-1, model_width), w_first, preferred_element_type=jnp.float32)
        ).astype(jnp.bfloat16)
        partial = jnp.dot(hidden, w_second, preferred_element_type=jnp.float32).astype(jnp.bfloat16)
        if k == 0:
            summed = partial.astype(jnp.float32)
        else:
            summed = summed + passed_along(partial, "y", n_y - k).astype(jnp.float32)
    back = lax.all_to_all(
        summed.astype(jnp.bfloat16).reshape(capacity, experts, model_width),
        "expert", split_axis=1, concat_axis=1, tiled=True,
    )
    return jnp.dot(
        combine_mat,
        back.reshape(capacity * experts, model_width).astype(jnp.float32),
        precision=lax.Precision.HIGHEST,
    )


def on_device(sent, norm_gain, router, w_in, w_out, expert_ids):
    arrived = passed_along(sent, "section", 1)[0]
    tok_count = arrived.shape[0]
    experts = router.shape[2]
    top_count = expert_ids.shape[2]
    capacity = max(2, (5 * top_count * tok_count + 4 * experts - 1) // (4 * experts))
    n_sec = lax.axis_size("section")
    n_zh = lax.axis_size("zh")
    crossed = [
        (s * n_zh + h, ((s + 1) % n_sec) * n_zh + (h + 1) % n_zh)
        for s in range(n_sec)
        for h in range(n_zh)
    ]
    partner_arrived = lax.ppermute(sent, ("section", "zh"), crossed)[0]
    normed = normalize(arrived, norm_gain[0])
    partner_rows = normalize(partner_arrived, norm_gain[0])
    own_pick = expert_ids[0]
    partner_pick = passed_along(own_pick, "zh", 1)
    w_first = w_in[0, 0]
    w_second = w_out[0, 0]
    own_slots, own_combine = dispatch(normed, own_pick, router[0], capacity)
    own_half = expert_pass(own_slots, own_combine, w_first, w_second)
    partner_slots, partner_combine = dispatch(partner_rows, partner_pick, router[0], capacity)
    partner_half = expert_pass(partner_slots, partner_combine, w_first, w_second)
    from_partner = passed_along(partner_half.astype(jnp.bfloat16), "zh", 1)
    combined = arrived.astype(jnp.float32) + own_half + from_partner.astype(jnp.float32)
    return passed_along(combined.astype(jnp.bfloat16)[None], "section", 1)


def solution(mesh):
    sizes = dict(mesh.shape)
    n_tensor = sizes["tensor"]
    fine = Mesh(
        mesh.devices.reshape(sizes["section"], sizes["expert"], n_tensor // 2, 2),
        ("section", "expert", "y", "zh"),
    )
    tokens = ("expert", "y", "zh")
    hidden_units = ("y", "zh")
    return jax.shard_map(
        on_device,
        mesh=fine,
        in_specs=(
            P("section", tokens, None),
            P("section", None),
            P("section", None, None),
            P("section", "expert", None, hidden_units),
            P("section", "expert", hidden_units, None),
            P("section", tokens, None),
        ),
        out_specs=P("section", tokens, None),
        check_vma=False,
    )
```

```python
import jax
import jax.numpy as jnp
from jax import lax
from jax.sharding import Mesh
from jax.sharding import PartitionSpec as P


def passed_along(value, axis, steps):
    count = lax.axis_size(axis)
    pairs = [(source, (source + steps) % count) for source in range(count)]
    return lax.ppermute(value, axis, pairs)


def normalize(inputs, gain_row):
    widened = inputs.astype(jnp.float32)
    mean_sq = jnp.mean(widened * widened, axis=-1, keepdims=True)
    return (widened * lax.rsqrt(mean_sq + 1e-05) * gain_row).astype(jnp.bfloat16)


def route(normed, router_mat, expert_pick, tok_block, capacity):
    logits = jnp.dot(normed, router_mat, preferred_element_type=jnp.float32)
    experts = router_mat.shape[1]
    labels = jnp.arange(experts, dtype=jnp.int32)
    pair_hot = (expert_pick[:, :, None] == labels[None, None, :]).astype(jnp.float32)
    picked = jnp.sum(pair_hot * logits[:, None, :], axis=-1)
    squashed = jax.nn.sigmoid(picked)
    gate_vals = squashed / jnp.sum(squashed, axis=-1, keepdims=True)
    blocks = expert_pick.shape[0] // tok_block
    pair_order = jnp.transpose(expert_pick.reshape(blocks, tok_block, 2), (0, 2, 1)).reshape(
        blocks, 2 * tok_block
    )
    one_hot = (pair_order[:, :, None] == labels[None, None, :]).astype(jnp.int32)
    before = jnp.cumsum(one_hot, axis=1) - one_hot
    pair_ranks = jnp.sum(before * one_hot, axis=-1)
    pair_ranks = jnp.transpose(pair_ranks.reshape(blocks, 2, tok_block), (0, 2, 1)).reshape(-1, 2)
    is_kept = pair_ranks < capacity
    return (gate_vals, pair_ranks, is_kept)


def dispatch(rows, pick, router_mat, capacity):
    tok_count, model_width = rows.shape
    experts = router_mat.shape[1]
    gate_vals, pair_ranks, is_kept = route(rows, router_mat, pick, tok_count, capacity)
    slot_ids = pair_ranks * experts + pick
    slot_count = experts * capacity
    slot_labels = jnp.arange(slot_count, dtype=jnp.int32)
    slot_hot = ((slot_ids[:, :, None] == slot_labels[None, None, :]) & is_kept[:, :, None]).astype(
        jnp.float32
    )
    placement = jnp.transpose(jnp.sum(slot_hot, axis=1)).astype(jnp.bfloat16)
    combine_mat = jnp.sum(slot_hot * gate_vals[:, :, None], axis=1)
    send_rows = jnp.dot(placement, rows, preferred_element_type=jnp.float32).astype(jnp.bfloat16)
    return send_rows.reshape(capacity, experts, model_width), combine_mat


def expert_pass(slot_grid, combine_mat, w_first, w_second):
    capacity, experts, model_width = slot_grid.shape
    n_y = lax.axis_size("y")
    received = lax.all_to_all(slot_grid, "expert", split_axis=1, concat_axis=1, tiled=True)
    copies = jnp.broadcast_to(received[None], (n_y,) + received.shape)
    rows_in = lax.all_to_all(copies, "y", split_axis=0, concat_axis=0, tiled=True)
    hidden = jax.nn.gelu(
        jnp.dot(rows_in.reshape(-1, model_width), w_first, preferred_element_type=jnp.float32)
    ).astype(jnp.bfloat16)
    partial = jnp.dot(hidden, w_second, preferred_element_type=jnp.float32).astype(jnp.bfloat16)
    partial = partial.reshape(n_y, capacity * experts, model_width)
    parts = lax.all_to_all(partial, "y", split_axis=0, concat_axis=0, tiled=True)
    summed = jnp.sum(parts.astype(jnp.float32), axis=0)
    back = lax.all_to_all(
        summed.astype(jnp.bfloat16).reshape(capacity, experts, model_width),
        "expert", split_axis=1, concat_axis=1, tiled=True,
    )
    return jnp.dot(
        combine_mat,
        back.reshape(capacity * experts, model_width).astype(jnp.float32),
        precision=lax.Precision.HIGHEST,
    )


def on_device(sent, norm_gain, router, w_in, w_out, expert_ids):
    arrived = passed_along(sent, "section", 1)[0]
    tok_count = arrived.shape[0]
    experts = router.shape[2]
    top_count = expert_ids.shape[2]
    capacity = max(2, (5 * top_count * tok_count + 4 * experts - 1) // (4 * experts))
    n_sec = lax.axis_size("section")
    n_zh = lax.axis_size("zh")
    crossed = [
        (s * n_zh + h, ((s + 1) % n_sec) * n_zh + (h + 1) % n_zh)
        for s in range(n_sec)
        for h in range(n_zh)
    ]
    partner_arrived = lax.ppermute(sent, ("section", "zh"), crossed)[0]
    normed = normalize(arrived, norm_gain[0])
    partner_rows = normalize(partner_arrived, norm_gain[0])
    own_pick = expert_ids[0]
    partner_pick = passed_along(own_pick, "zh", 1)
    w_first = w_in[0, 0]
    w_second = w_out[0, 0]
    own_slots, own_combine = dispatch(normed, own_pick, router[0], capacity)
    own_half = expert_pass(own_slots, own_combine, w_first, w_second)
    partner_slots, partner_combine = dispatch(partner_rows, partner_pick, router[0], capacity)
    partner_half = expert_pass(partner_slots, partner_combine, w_first, w_second)
    from_partner = passed_along(partner_half.astype(jnp.bfloat16), "zh", 1)
    combined = arrived.astype(jnp.float32) + own_half + from_partner.astype(jnp.float32)
    return passed_along(combined.astype(jnp.bfloat16)[None], "section", 1)


def solution(mesh):
    sizes = dict(mesh.shape)
    n_tensor = sizes["tensor"]
    fine = Mesh(
        mesh.devices.reshape(sizes["section"], sizes["expert"], n_tensor // 2, 2),
        ("section", "expert", "y", "zh"),
    )
    tokens = ("expert", "y", "zh")
    hidden_units = ("y", "zh")
    return jax.shard_map(
        on_device,
        mesh=fine,
        in_specs=(
            P("section", tokens, None),
            P("section", None),
            P("section", None, None),
            P("section", "expert", None, hidden_units),
            P("section", "expert", hidden_units, None),
            P("section", tokens, None),
        ),
        out_specs=P("section", tokens, None),
        check_vma=False,
    )
```

```python
import jax
import jax.numpy as jnp
from jax import lax
from jax.sharding import Mesh
from jax.sharding import PartitionSpec as P


def passed_along(value, axis, steps):
    count = lax.axis_size(axis)
    pairs = [(source, (source + steps) % count) for source in range(count)]
    return lax.ppermute(value, axis, pairs)


def normalize(inputs, gain_row):
    widened = inputs.astype(jnp.float32)
    mean_sq = jnp.mean(widened * widened, axis=-1, keepdims=True)
    return (widened * lax.rsqrt(mean_sq + 1e-05) * gain_row).astype(jnp.bfloat16)


def route(normed, router_mat, expert_pick, tok_block, capacity):
    logits = jnp.dot(normed, router_mat, preferred_element_type=jnp.float32)
    experts = router_mat.shape[1]
    labels = jnp.arange(experts, dtype=jnp.int32)
    pair_hot = (expert_pick[:, :, None] == labels[None, None, :]).astype(jnp.float32)
    picked = jnp.sum(pair_hot * logits[:, None, :], axis=-1)
    squashed = jax.nn.sigmoid(picked)
    gate_vals = squashed / jnp.sum(squashed, axis=-1, keepdims=True)
    blocks = expert_pick.shape[0] // tok_block
    pair_order = jnp.transpose(expert_pick.reshape(blocks, tok_block, 2), (0, 2, 1)).reshape(
        blocks, 2 * tok_block
    )
    one_hot = (pair_order[:, :, None] == labels[None, None, :]).astype(jnp.int32)
    before = jnp.cumsum(one_hot, axis=1) - one_hot
    pair_ranks = jnp.sum(before * one_hot, axis=-1)
    pair_ranks = jnp.transpose(pair_ranks.reshape(blocks, 2, tok_block), (0, 2, 1)).reshape(-1, 2)
    is_kept = pair_ranks < capacity
    return (gate_vals, pair_ranks, is_kept)


def dispatch(rows, pick, router_mat, capacity):
    tok_count, model_width = rows.shape
    experts = router_mat.shape[1]
    gate_vals, pair_ranks, is_kept = route(rows, router_mat, pick, tok_count, capacity)
    slot_ids = pair_ranks * experts + pick
    slot_count = experts * capacity
    slot_labels = jnp.arange(slot_count, dtype=jnp.int32)
    slot_hot = ((slot_ids[:, :, None] == slot_labels[None, None, :]) & is_kept[:, :, None]).astype(
        jnp.float32
    )
    placement = jnp.transpose(jnp.sum(slot_hot, axis=1)).astype(jnp.bfloat16)
    combine_mat = jnp.sum(slot_hot * gate_vals[:, :, None], axis=1)
    send_rows = jnp.dot(placement, rows, preferred_element_type=jnp.float32).astype(jnp.bfloat16)
    return send_rows.reshape(capacity, experts, model_width), combine_mat


def expert_pass(slot_grid, combine_mat, w_first, w_second):
    capacity, experts, model_width = slot_grid.shape
    n_y = lax.axis_size("y")
    received = lax.all_to_all(slot_grid, "expert", split_axis=1, concat_axis=1, tiled=True)
    gathered = lax.all_gather(received, "y", axis=0, tiled=False)
    hidden = jax.nn.gelu(
        jnp.dot(gathered.reshape(-1, model_width), w_first, preferred_element_type=jnp.float32)
    ).astype(jnp.bfloat16)
    partial = jnp.dot(hidden, w_second, preferred_element_type=jnp.float32).astype(jnp.bfloat16)
    partial = partial.reshape(n_y, capacity * experts, model_width)
    me = lax.axis_index("y")
    summed = lax.dynamic_index_in_dim(partial, me, axis=0, keepdims=False).astype(jnp.float32)
    for k in range(1, n_y):
        block = lax.dynamic_index_in_dim(partial, (me + k) % n_y, axis=0, keepdims=False)
        summed = summed + passed_along(block, "y", k).astype(jnp.float32)
    back = lax.all_to_all(
        summed.astype(jnp.bfloat16).reshape(capacity, experts, model_width),
        "expert", split_axis=1, concat_axis=1, tiled=True,
    )
    return jnp.dot(
        combine_mat,
        back.reshape(capacity * experts, model_width).astype(jnp.float32),
        precision=lax.Precision.HIGHEST,
    )


def on_device(sent, norm_gain, router, w_in, w_out, expert_ids):
    arrived = passed_along(sent, "section", 1)[0]
    tok_count = arrived.shape[0]
    experts = router.shape[2]
    top_count = expert_ids.shape[2]
    capacity = max(2, (5 * top_count * tok_count + 4 * experts - 1) // (4 * experts))
    n_sec = lax.axis_size("section")
    n_zh = lax.axis_size("zh")
    crossed = [
        (s * n_zh + h, ((s + 1) % n_sec) * n_zh + (h + 1) % n_zh)
        for s in range(n_sec)
        for h in range(n_zh)
    ]
    partner_arrived = lax.ppermute(sent, ("section", "zh"), crossed)[0]
    normed = normalize(arrived, norm_gain[0])
    partner_rows = normalize(partner_arrived, norm_gain[0])
    own_pick = expert_ids[0]
    partner_pick = passed_along(own_pick, "zh", 1)
    w_first = w_in[0, 0]
    w_second = w_out[0, 0]
    own_slots, own_combine = dispatch(normed, own_pick, router[0], capacity)
    own_half = expert_pass(own_slots, own_combine, w_first, w_second)
    partner_slots, partner_combine = dispatch(partner_rows, partner_pick, router[0], capacity)
    partner_half = expert_pass(partner_slots, partner_combine, w_first, w_second)
    from_partner = passed_along(partner_half.astype(jnp.bfloat16), "zh", 1)
    combined = arrived.astype(jnp.float32) + own_half + from_partner.astype(jnp.float32)
    return passed_along(combined.astype(jnp.bfloat16)[None], "section", 1)


def solution(mesh):
    sizes = dict(mesh.shape)
    n_tensor = sizes["tensor"]
    fine = Mesh(
        mesh.devices.reshape(sizes["section"], sizes["expert"], n_tensor // 2, 2),
        ("section", "expert", "y", "zh"),
    )
    tokens = ("expert", "y", "zh")
    hidden_units = ("y", "zh")
    return jax.shard_map(
        on_device,
        mesh=fine,
        in_specs=(
            P("section", tokens, None),
            P("section", None),
            P("section", None, None),
            P("section", "expert", None, hidden_units),
            P("section", "expert", hidden_units, None),
            P("section", tokens, None),
        ),
        out_specs=P("section", tokens, None),
        check_vma=False,
    )
```

```python
import jax
import jax.numpy as jnp
from jax import lax
from jax.sharding import Mesh
from jax.sharding import PartitionSpec as P

TOK_BLOCK = 16
QUARTER = ("r", "x")


def passed_along(value, axis, steps):
    count = lax.axis_size(axis)
    pairs = [(source, (source + steps) % count) for source in range(count)]
    return lax.ppermute(value, axis, pairs)


def normalize(inputs, gain_row):
    widened = inputs.astype(jnp.float32)
    mean_sq = jnp.mean(widened * widened, axis=-1, keepdims=True)
    return (widened * lax.rsqrt(mean_sq + 1e-05) * gain_row).astype(jnp.bfloat16)


def route(normed, router_mat, expert_pick, tok_block, capacity):
    logits = jnp.dot(normed, router_mat, preferred_element_type=jnp.float32)
    experts = router_mat.shape[1]
    labels = jnp.arange(experts, dtype=jnp.int32)
    pair_hot = (expert_pick[:, :, None] == labels[None, None, :]).astype(jnp.float32)
    picked = jnp.sum(pair_hot * logits[:, None, :], axis=-1)
    squashed = jax.nn.sigmoid(picked)
    gate_vals = squashed / jnp.sum(squashed, axis=-1, keepdims=True)
    blocks = expert_pick.shape[0] // tok_block
    pair_order = jnp.transpose(expert_pick.reshape(blocks, tok_block, 2), (0, 2, 1)).reshape(
        blocks, 2 * tok_block
    )
    one_hot = (pair_order[:, :, None] == labels[None, None, :]).astype(jnp.int32)
    before = jnp.cumsum(one_hot, axis=1) - one_hot
    pair_ranks = jnp.sum(before * one_hot, axis=-1)
    pair_ranks = jnp.transpose(pair_ranks.reshape(blocks, 2, tok_block), (0, 2, 1)).reshape(-1, 2)
    is_kept = pair_ranks < capacity
    return (gate_vals, pair_ranks, is_kept)


def dispatch(rows, pick, router_mat, capacity, home_q, n_local):
    tok_count, model_width = rows.shape
    tok_block = TOK_BLOCK
    blocks = tok_count // tok_block
    gate_vals, pair_ranks, is_kept = route(rows, router_mat, pick, tok_block, capacity)
    block_of = (jnp.arange(tok_count, dtype=jnp.int32) // tok_block)[:, None]
    here = is_kept & (pick // n_local == home_q)
    slot_ids = (block_of * capacity + pair_ranks) * n_local + pick % n_local
    slot_count = blocks * capacity * n_local
    slot_labels = jnp.arange(slot_count, dtype=jnp.int32)
    slot_hot = ((slot_ids[:, :, None] == slot_labels[None, None, :]) & here[:, :, None]).astype(
        jnp.float32
    )
    placement = jnp.transpose(jnp.sum(slot_hot, axis=1)).astype(jnp.bfloat16)
    combine_mat = jnp.sum(slot_hot * gate_vals[:, :, None], axis=1)
    send_rows = jnp.dot(placement, rows, preferred_element_type=jnp.float32).astype(jnp.bfloat16)
    return send_rows.reshape(blocks * capacity, n_local, model_width), combine_mat


def expert_pass(slot_grid, combine_mat, w_first, w_second):
    lead, n_local, model_width = slot_grid.shape
    n_y = lax.axis_size("y")
    received = lax.all_to_all(slot_grid, QUARTER, split_axis=1, concat_axis=1, tiled=True)
    summed = None
    for k in range(n_y):
        rows_in = received if k == 0 else passed_along(received, "y", k)
        hidden = jax.nn.gelu(
            jnp.dot(rows_in.reshape(-1, model_width), w_first, preferred_element_type=jnp.float32)
        ).astype(jnp.bfloat16)
        partial = jnp.dot(hidden, w_second, preferred_element_type=jnp.float32).astype(jnp.bfloat16)
        if k == 0:
            summed = partial.astype(jnp.float32)
        else:
            summed = summed + passed_along(partial, "y", n_y - k).astype(jnp.float32)
    back = lax.all_to_all(
        summed.astype(jnp.bfloat16).reshape(lead, n_local, model_width),
        QUARTER, split_axis=1, concat_axis=1, tiled=True,
    )
    return jnp.dot(
        combine_mat,
        back.reshape(lead * n_local, model_width).astype(jnp.float32),
        precision=lax.Precision.HIGHEST,
    )


def shifted_pairs(sizes, steps):
    total = 1
    for size in sizes:
        total *= size
    pairs = []
    for source in range(total):
        digits, rest = [], source
        for size in reversed(sizes):
            digits.append(rest % size)
            rest //= size
        digits = digits[::-1]
        dest = 0
        for digit, size, step in zip(digits, sizes, steps):
            dest = dest * size + (digit + step) % size
        pairs.append((source, dest))
    return pairs


def on_device(sent, norm_gain, router, w_in, w_out, expert_ids):
    arrived = passed_along(sent, "section", 1)[0]
    tok_count = arrived.shape[0]
    experts = router.shape[2]
    top_count = expert_ids.shape[2]
    capacity = max(2, (5 * top_count * tok_count + 4 * experts - 1) // (4 * experts))
    n_sec, n_q, n_zh = (lax.axis_size(a) for a in ("section", "q2", "zh"))
    n_local = experts // n_q
    home_q = lax.axis_index("q2")
    offsets = [(a, c) for a in range(n_q) for c in range(n_zh) if (a, c) != (0, 0)]
    rows = [normalize(arrived, norm_gain[0])]
    picks = [expert_ids[0]]
    for a, c in offsets:
        far = lax.ppermute(sent, ("section", "q2", "zh"), shifted_pairs((n_sec, n_q, n_zh), (1, a, c)))
        rows.append(normalize(far[0], norm_gain[0]))
        picks.append(lax.ppermute(expert_ids[0], ("q2", "zh"), shifted_pairs((n_q, n_zh), (a, c))))
    w_first = w_in[0, 0]
    w_second = w_out[0, 0]
    chunk = len(rows) // 2
    halves = []
    for part in (slice(0, chunk), slice(chunk, len(rows))):
        slots, combine = dispatch(
            jnp.concatenate(rows[part], axis=0), jnp.concatenate(picks[part], axis=0),
            router[0], capacity, home_q, n_local,
        )
        halves.append(expert_pass(slots, combine, w_first, w_second))
    sums = jnp.concatenate(halves, axis=0).reshape(len(rows), tok_count, -1)
    combined = arrived.astype(jnp.float32) + sums[0]
    for j, (a, c) in enumerate(offsets, start=1):
        home = shifted_pairs((n_q, n_zh), (-a, -c))
        combined = combined + lax.ppermute(sums[j].astype(jnp.bfloat16), ("q2", "zh"), home).astype(
            jnp.float32
        )
    return passed_along(combined.astype(jnp.bfloat16)[None], "section", 1)


def solution(mesh):
    sizes = dict(mesh.shape)
    n_expert, n_tensor = sizes["expert"], sizes["tensor"]
    n_x = 4
    fine = Mesh(
        mesh.devices.reshape(sizes["section"], 2, n_expert // (2 * n_x), n_x, n_tensor // 2, 2),
        ("section", "q2", "r", "x", "y", "zh"),
    )
    experts_at = ("q2", "r", "x")
    hidden_units = ("y", "zh")
    tokens = experts_at + hidden_units
    return jax.shard_map(
        on_device,
        mesh=fine,
        in_specs=(
            P("section", tokens, None),
            P("section", None),
            P("section", None, None),
            P("section", experts_at, None, hidden_units),
            P("section", experts_at, hidden_units, None),
            P("section", tokens, None),
        ),
        out_specs=P("section", tokens, None),
        check_vma=False,
    )
```

```python
import jax
import jax.numpy as jnp
from jax import lax
from jax.sharding import Mesh
from jax.sharding import PartitionSpec as P

TOK_BLOCK = 16
QUARTER = ("r", "x")


def passed_along(value, axis, steps):
    count = lax.axis_size(axis)
    pairs = [(source, (source + steps) % count) for source in range(count)]
    return lax.ppermute(value, axis, pairs)


def normalize(inputs, gain_row):
    widened = inputs.astype(jnp.float32)
    mean_sq = jnp.mean(widened * widened, axis=-1, keepdims=True)
    return (widened * lax.rsqrt(mean_sq + 1e-05) * gain_row).astype(jnp.bfloat16)


def route(normed, router_mat, expert_pick, tok_block, capacity):
    logits = jnp.dot(normed, router_mat, preferred_element_type=jnp.float32)
    experts = router_mat.shape[1]
    labels = jnp.arange(experts, dtype=jnp.int32)
    pair_hot = (expert_pick[:, :, None] == labels[None, None, :]).astype(jnp.float32)
    picked = jnp.sum(pair_hot * logits[:, None, :], axis=-1)
    squashed = jax.nn.sigmoid(picked)
    gate_vals = squashed / jnp.sum(squashed, axis=-1, keepdims=True)
    blocks = expert_pick.shape[0] // tok_block
    pair_order = jnp.transpose(expert_pick.reshape(blocks, tok_block, 2), (0, 2, 1)).reshape(
        blocks, 2 * tok_block
    )
    one_hot = (pair_order[:, :, None] == labels[None, None, :]).astype(jnp.int32)
    before = jnp.cumsum(one_hot, axis=1) - one_hot
    pair_ranks = jnp.sum(before * one_hot, axis=-1)
    pair_ranks = jnp.transpose(pair_ranks.reshape(blocks, 2, tok_block), (0, 2, 1)).reshape(-1, 2)
    is_kept = pair_ranks < capacity
    return (gate_vals, pair_ranks, is_kept)


def dispatch(rows, pick, router_mat, capacity, home_q, n_local):
    tok_count, model_width = rows.shape
    tok_block = TOK_BLOCK
    blocks = tok_count // tok_block
    gate_vals, pair_ranks, is_kept = route(rows, router_mat, pick, tok_block, capacity)
    block_of = (jnp.arange(tok_count, dtype=jnp.int32) // tok_block)[:, None]
    here = is_kept & (pick // n_local == home_q)
    slot_ids = (block_of * capacity + pair_ranks) * n_local + pick % n_local
    slot_count = blocks * capacity * n_local
    slot_labels = jnp.arange(slot_count, dtype=jnp.int32)
    slot_hot = ((slot_ids[:, :, None] == slot_labels[None, None, :]) & here[:, :, None]).astype(
        jnp.float32
    )
    placement = jnp.transpose(jnp.sum(slot_hot, axis=1)).astype(jnp.bfloat16)
    combine_mat = jnp.sum(slot_hot * gate_vals[:, :, None], axis=1)
    send_rows = jnp.dot(placement, rows, preferred_element_type=jnp.float32).astype(jnp.bfloat16)
    return send_rows.reshape(blocks * capacity, n_local, model_width), combine_mat


def expert_pass(slot_grid, combine_mat, w_first, w_second):
    lead, n_local, model_width = slot_grid.shape
    n_y = lax.axis_size("y")
    received = lax.all_to_all(slot_grid, QUARTER, split_axis=1, concat_axis=1, tiled=True)
    summed = None
    for k in range(n_y):
        rows_in = received if k == 0 else passed_along(received, "y", k)
        hidden = jax.nn.gelu(
            jnp.dot(rows_in.reshape(-1, model_width), w_first, preferred_element_type=jnp.float32)
        ).astype(jnp.bfloat16)
        partial = jnp.dot(hidden, w_second, preferred_element_type=jnp.float32).astype(jnp.bfloat16)
        if k == 0:
            summed = partial.astype(jnp.float32)
        else:
            summed = summed + passed_along(partial, "y", n_y - k).astype(jnp.float32)
    back = lax.all_to_all(
        summed.astype(jnp.bfloat16).reshape(lead, n_local, model_width),
        QUARTER, split_axis=1, concat_axis=1, tiled=True,
    )
    return jnp.dot(
        combine_mat,
        back.reshape(lead * n_local, model_width).astype(jnp.float32),
        precision=lax.Precision.HIGHEST,
    )


def shifted_pairs(sizes, steps):
    total = 1
    for size in sizes:
        total *= size
    pairs = []
    for source in range(total):
        digits, rest = [], source
        for size in reversed(sizes):
            digits.append(rest % size)
            rest //= size
        digits = digits[::-1]
        dest = 0
        for digit, size, step in zip(digits, sizes, steps):
            dest = dest * size + (digit + step) % size
        pairs.append((source, dest))
    return pairs


def on_device(sent, norm_gain, router, w_in, w_out, expert_ids):
    arrived = passed_along(sent, "section", 1)[0]
    tok_count = arrived.shape[0]
    experts = router.shape[2]
    top_count = expert_ids.shape[2]
    capacity = max(2, (5 * top_count * tok_count + 4 * experts - 1) // (4 * experts))
    n_sec, n_q, n_zh = (lax.axis_size(a) for a in ("section", "q2", "zh"))
    n_local = experts // n_q
    home_q = lax.axis_index("q2")
    offsets = sorted(
        ((a, c) for a in range(n_q) for c in range(n_zh) if (a, c) != (0, 0)),
        key=lambda step: (step[1], -step[0]),
    )
    rows = [normalize(arrived, norm_gain[0])]
    picks = [expert_ids[0]]
    for a, c in offsets:
        far = lax.ppermute(sent, ("section", "q2", "zh"), shifted_pairs((n_sec, n_q, n_zh), (1, a, c)))
        rows.append(normalize(far[0], norm_gain[0]))
        picks.append(lax.ppermute(expert_ids[0], ("q2", "zh"), shifted_pairs((n_q, n_zh), (a, c))))
    w_first = w_in[0, 0]
    w_second = w_out[0, 0]
    chunk = len(rows) // 2
    halves = []
    for part in (slice(0, chunk), slice(chunk, len(rows))):
        slots, combine = dispatch(
            jnp.concatenate(rows[part], axis=0), jnp.concatenate(picks[part], axis=0),
            router[0], capacity, home_q, n_local,
        )
        halves.append(expert_pass(slots, combine, w_first, w_second))
    sums = jnp.concatenate(halves, axis=0).reshape(len(rows), tok_count, -1)
    combined = arrived.astype(jnp.float32) + sums[0]
    for j, (a, c) in enumerate(offsets, start=1):
        home = shifted_pairs((n_q, n_zh), (-a, -c))
        combined = combined + lax.ppermute(sums[j].astype(jnp.bfloat16), ("q2", "zh"), home).astype(
            jnp.float32
        )
    return passed_along(combined.astype(jnp.bfloat16)[None], "section", 1)


def solution(mesh):
    sizes = dict(mesh.shape)
    n_expert, n_tensor = sizes["expert"], sizes["tensor"]
    n_x = 4
    fine = Mesh(
        mesh.devices.reshape(sizes["section"], 2, n_expert // (2 * n_x), n_x, n_tensor // 2, 2),
        ("section", "q2", "r", "x", "y", "zh"),
    )
    experts_at = ("q2", "r", "x")
    hidden_units = ("y", "zh")
    tokens = experts_at + hidden_units
    return jax.shard_map(
        on_device,
        mesh=fine,
        in_specs=(
            P("section", tokens, None),
            P("section", None),
            P("section", None, None),
            P("section", experts_at, None, hidden_units),
            P("section", experts_at, hidden_units, None),
            P("section", tokens, None),
        ),
        out_specs=P("section", tokens, None),
        check_vma=False,
    )
```

```python
import jax
import jax.numpy as jnp
from jax import lax
from jax.sharding import Mesh
from jax.sharding import PartitionSpec as P


def passed_along(value, axis, steps):
    count = lax.axis_size(axis)
    pairs = [(source, (source + steps) % count) for source in range(count)]
    return lax.ppermute(value, axis, pairs)


def swapped(value, axis, mask):
    count = lax.axis_size(axis)
    return lax.ppermute(value, axis, [(source, source ^ mask) for source in range(count)])


def normalize(inputs, gain_row):
    widened = inputs.astype(jnp.float32)
    mean_sq = jnp.mean(widened * widened, axis=-1, keepdims=True)
    return (widened * lax.rsqrt(mean_sq + 1e-05) * gain_row).astype(jnp.bfloat16)


def route(normed, router_mat, expert_pick, tok_block, capacity):
    logits = jnp.dot(normed, router_mat, preferred_element_type=jnp.float32)
    experts = router_mat.shape[1]
    labels = jnp.arange(experts, dtype=jnp.int32)
    pair_hot = (expert_pick[:, :, None] == labels[None, None, :]).astype(jnp.float32)
    picked = jnp.sum(pair_hot * logits[:, None, :], axis=-1)
    squashed = jax.nn.sigmoid(picked)
    gate_vals = squashed / jnp.sum(squashed, axis=-1, keepdims=True)
    blocks = expert_pick.shape[0] // tok_block
    pair_order = jnp.transpose(expert_pick.reshape(blocks, tok_block, 2), (0, 2, 1)).reshape(
        blocks, 2 * tok_block
    )
    one_hot = (pair_order[:, :, None] == labels[None, None, :]).astype(jnp.int32)
    before = jnp.cumsum(one_hot, axis=1) - one_hot
    pair_ranks = jnp.sum(before * one_hot, axis=-1)
    pair_ranks = jnp.transpose(pair_ranks.reshape(blocks, 2, tok_block), (0, 2, 1)).reshape(-1, 2)
    is_kept = pair_ranks < capacity
    return (gate_vals, pair_ranks, is_kept)


def dispatch(rows, pick, router_mat, capacity):
    tok_count, model_width = rows.shape
    experts = router_mat.shape[1]
    gate_vals, pair_ranks, is_kept = route(rows, router_mat, pick, tok_count, capacity)
    slot_ids = pair_ranks * experts + pick
    slot_count = experts * capacity
    slot_labels = jnp.arange(slot_count, dtype=jnp.int32)
    slot_hot = ((slot_ids[:, :, None] == slot_labels[None, None, :]) & is_kept[:, :, None]).astype(
        jnp.float32
    )
    placement = jnp.transpose(jnp.sum(slot_hot, axis=1)).astype(jnp.bfloat16)
    combine_mat = jnp.sum(slot_hot * gate_vals[:, :, None], axis=1)
    send_rows = jnp.dot(placement, rows, preferred_element_type=jnp.float32).astype(jnp.bfloat16)
    return send_rows.reshape(capacity, experts, model_width), combine_mat


def expert_pass(slot_grid, combine_mat, w_first, w_second):
    capacity, experts, model_width = slot_grid.shape
    n_y = lax.axis_size("y")
    received = lax.all_to_all(slot_grid, "expert", split_axis=1, concat_axis=1, tiled=True)
    def ffn(rows_in):
        hidden = jax.nn.gelu(
            jnp.dot(rows_in.reshape(-1, model_width), w_first, preferred_element_type=jnp.float32)
        ).astype(jnp.bfloat16)
        return jnp.dot(hidden, w_second, preferred_element_type=jnp.float32).astype(jnp.bfloat16)

    near = swapped(received, "y", 1)
    pair = jnp.stack([received, near])
    far = swapped(pair, "y", 2)
    own_part = ffn(received)
    near_part = ffn(near)
    far_part = ffn(far).reshape(2, -1, model_width)
    far_back = swapped(far_part, "y", 2)
    summed = own_part.astype(jnp.float32) + far_back[0].astype(jnp.float32)
    near_sum = near_part.astype(jnp.float32) + far_back[1].astype(jnp.float32)
    summed = summed + swapped(near_sum.astype(jnp.bfloat16), "y", 1).astype(jnp.float32)
    back = lax.all_to_all(
        summed.astype(jnp.bfloat16).reshape(capacity, experts, model_width),
        "expert", split_axis=1, concat_axis=1, tiled=True,
    )
    return jnp.dot(
        combine_mat,
        back.reshape(capacity * experts, model_width).astype(jnp.float32),
        precision=lax.Precision.HIGHEST,
    )


def on_device(sent, norm_gain, router, w_in, w_out, expert_ids):
    arrived = passed_along(sent, "section", 1)[0]
    tok_count = arrived.shape[0]
    experts = router.shape[2]
    top_count = expert_ids.shape[2]
    capacity = max(2, (5 * top_count * tok_count + 4 * experts - 1) // (4 * experts))
    n_sec = lax.axis_size("section")
    n_zh = lax.axis_size("zh")
    crossed = [
        (s * n_zh + h, ((s + 1) % n_sec) * n_zh + (h + 1) % n_zh)
        for s in range(n_sec)
        for h in range(n_zh)
    ]
    partner_arrived = lax.ppermute(sent, ("section", "zh"), crossed)[0]
    normed = normalize(arrived, norm_gain[0])
    partner_rows = normalize(partner_arrived, norm_gain[0])
    own_pick = expert_ids[0]
    partner_pick = passed_along(own_pick, "zh", 1)
    w_first = w_in[0, 0]
    w_second = w_out[0, 0]
    own_slots, own_combine = dispatch(normed, own_pick, router[0], capacity)
    own_half = expert_pass(own_slots, own_combine, w_first, w_second)
    partner_slots, partner_combine = dispatch(partner_rows, partner_pick, router[0], capacity)
    partner_half = expert_pass(partner_slots, partner_combine, w_first, w_second)
    from_partner = passed_along(partner_half.astype(jnp.bfloat16), "zh", 1)
    combined = arrived.astype(jnp.float32) + own_half + from_partner.astype(jnp.float32)
    return passed_along(combined.astype(jnp.bfloat16)[None], "section", 1)


def solution(mesh):
    sizes = dict(mesh.shape)
    n_tensor = sizes["tensor"]
    fine = Mesh(
        mesh.devices.reshape(sizes["section"], sizes["expert"], n_tensor // 2, 2),
        ("section", "expert", "y", "zh"),
    )
    tokens = ("expert", "y", "zh")
    hidden_units = ("y", "zh")
    return jax.shard_map(
        on_device,
        mesh=fine,
        in_specs=(
            P("section", tokens, None),
            P("section", None),
            P("section", None, None),
            P("section", "expert", None, hidden_units),
            P("section", "expert", hidden_units, None),
            P("section", tokens, None),
        ),
        out_specs=P("section", tokens, None),
        check_vma=False,
    )
```

```python
import jax
import jax.numpy as jnp
from jax import lax
from jax.sharding import Mesh
from jax.sharding import PartitionSpec as P

TOK_BLOCK = 16
QUARTER = ("r", "x")


def passed_along(value, axis, steps):
    count = lax.axis_size(axis)
    pairs = [(source, (source + steps) % count) for source in range(count)]
    return lax.ppermute(value, axis, pairs)


def normalize(inputs, gain_row):
    widened = inputs.astype(jnp.float32)
    mean_sq = jnp.mean(widened * widened, axis=-1, keepdims=True)
    return (widened * lax.rsqrt(mean_sq + 1e-05) * gain_row).astype(jnp.bfloat16)


def route(normed, router_mat, expert_pick, tok_block, capacity):
    logits = jnp.dot(normed, router_mat, preferred_element_type=jnp.float32)
    experts = router_mat.shape[1]
    labels = jnp.arange(experts, dtype=jnp.int32)
    pair_hot = (expert_pick[:, :, None] == labels[None, None, :]).astype(jnp.float32)
    picked = jnp.sum(pair_hot * logits[:, None, :], axis=-1)
    squashed = jax.nn.sigmoid(picked)
    gate_vals = squashed / jnp.sum(squashed, axis=-1, keepdims=True)
    blocks = expert_pick.shape[0] // tok_block
    pair_order = jnp.transpose(expert_pick.reshape(blocks, tok_block, 2), (0, 2, 1)).reshape(
        blocks, 2 * tok_block
    )
    one_hot = (pair_order[:, :, None] == labels[None, None, :]).astype(jnp.int32)
    before = jnp.cumsum(one_hot, axis=1) - one_hot
    pair_ranks = jnp.sum(before * one_hot, axis=-1)
    pair_ranks = jnp.transpose(pair_ranks.reshape(blocks, 2, tok_block), (0, 2, 1)).reshape(-1, 2)
    is_kept = pair_ranks < capacity
    return (gate_vals, pair_ranks, is_kept)


def dispatch(rows, pick, router_mat, capacity, home_q, n_local):
    tok_count, model_width = rows.shape
    tok_block = TOK_BLOCK
    blocks = tok_count // tok_block
    gate_vals, pair_ranks, is_kept = route(rows, router_mat, pick, tok_block, capacity)
    block_of = (jnp.arange(tok_count, dtype=jnp.int32) // tok_block)[:, None]
    here = is_kept & (pick // n_local == home_q)
    slot_ids = (block_of * capacity + pair_ranks) * n_local + pick % n_local
    slot_count = blocks * capacity * n_local
    slot_labels = jnp.arange(slot_count, dtype=jnp.int32)
    slot_hot = ((slot_ids[:, :, None] == slot_labels[None, None, :]) & here[:, :, None]).astype(
        jnp.float32
    )
    placement = jnp.transpose(jnp.sum(slot_hot, axis=1)).astype(jnp.bfloat16)
    combine_mat = jnp.sum(slot_hot * gate_vals[:, :, None], axis=1)
    send_rows = jnp.dot(placement, rows, preferred_element_type=jnp.float32).astype(jnp.bfloat16)
    return send_rows.reshape(blocks * capacity, n_local, model_width), combine_mat


def expert_pass(slot_grid, combine_mat, w_first, w_second):
    lead, n_local, model_width = slot_grid.shape
    n_y = lax.axis_size("y")
    received = lax.all_to_all(slot_grid, QUARTER, split_axis=1, concat_axis=1, tiled=True)
    summed = None
    for k in range(n_y):
        rows_in = received if k == 0 else passed_along(received, "y", k)
        hidden = jax.nn.gelu(
            jnp.dot(rows_in.reshape(-1, model_width), w_first, preferred_element_type=jnp.float32)
        ).astype(jnp.bfloat16)
        partial = jnp.dot(hidden, w_second, preferred_element_type=jnp.float32).astype(jnp.bfloat16)
        if k == 0:
            summed = partial.astype(jnp.float32)
        else:
            summed = summed + passed_along(partial, "y", n_y - k).astype(jnp.float32)
    back = lax.all_to_all(
        summed.astype(jnp.bfloat16).reshape(lead, n_local, model_width),
        QUARTER, split_axis=1, concat_axis=1, tiled=True,
    )
    return jnp.dot(
        combine_mat,
        back.reshape(lead * n_local, model_width).astype(jnp.float32),
        precision=lax.Precision.HIGHEST,
    )


def shifted_pairs(sizes, steps):
    total = 1
    for size in sizes:
        total *= size
    pairs = []
    for source in range(total):
        digits, rest = [], source
        for size in reversed(sizes):
            digits.append(rest % size)
            rest //= size
        digits = digits[::-1]
        dest = 0
        for digit, size, step in zip(digits, sizes, steps):
            dest = dest * size + (digit + step) % size
        pairs.append((source, dest))
    return pairs


def on_device(sent, norm_gain, router, w_in, w_out, expert_ids):
    arrived = passed_along(sent, "section", 1)[0]
    tok_count = arrived.shape[0]
    experts = router.shape[2]
    top_count = expert_ids.shape[2]
    capacity = max(2, (5 * top_count * tok_count + 4 * experts - 1) // (4 * experts))
    n_sec, n_q, n_zh = (lax.axis_size(a) for a in ("section", "q2", "zh"))
    n_local = experts // n_q
    home_q = lax.axis_index("q2")
    offsets = sorted(
        ((a, c) for a in range(n_q) for c in range(n_zh) if (a, c) != (0, 0)),
        key=lambda step: (step[1], -step[0]),
    )
    normed = normalize(arrived, norm_gain[0])
    own_pick = expert_ids[0]
    model_width = normed.shape[1]
    lanes = 128
    tag = jnp.pad(own_pick.astype(jnp.bfloat16), ((0, 0), (0, lanes - top_count)))
    packed = jnp.concatenate([normed, tag], axis=1)
    rows = [normed]
    picks = [own_pick]
    for a, c in offsets:
        far = lax.ppermute(packed, ("q2", "zh"), shifted_pairs((n_q, n_zh), (a, c)))
        rows.append(far[:, :model_width])
        picks.append(far[:, model_width:model_width + top_count].astype(jnp.int32))
    w_first = w_in[0, 0]
    w_second = w_out[0, 0]
    chunk = len(rows) // 2
    halves = []
    for part in (slice(0, chunk), slice(chunk, len(rows))):
        slots, combine = dispatch(
            jnp.concatenate(rows[part], axis=0), jnp.concatenate(picks[part], axis=0),
            router[0], capacity, home_q, n_local,
        )
        halves.append(expert_pass(slots, combine, w_first, w_second))
    sums = jnp.concatenate(halves, axis=0).reshape(len(rows), tok_count, -1)
    combined = arrived.astype(jnp.float32) + sums[0]
    for j, (a, c) in enumerate(offsets, start=1):
        home = shifted_pairs((n_q, n_zh), (-a, -c))
        combined = combined + lax.ppermute(sums[j].astype(jnp.bfloat16), ("q2", "zh"), home).astype(
            jnp.float32
        )
    return passed_along(combined.astype(jnp.bfloat16)[None], "section", 1)


def solution(mesh):
    sizes = dict(mesh.shape)
    n_expert, n_tensor = sizes["expert"], sizes["tensor"]
    n_x = 4
    fine = Mesh(
        mesh.devices.reshape(sizes["section"], 2, n_expert // (2 * n_x), n_x, n_tensor // 2, 2),
        ("section", "q2", "r", "x", "y", "zh"),
    )
    experts_at = ("q2", "r", "x")
    hidden_units = ("y", "zh")
    tokens = experts_at + hidden_units
    return jax.shard_map(
        on_device,
        mesh=fine,
        in_specs=(
            P("section", tokens, None),
            P("section", None),
            P("section", None, None),
            P("section", experts_at, None, hidden_units),
            P("section", experts_at, hidden_units, None),
            P("section", tokens, None),
        ),
        out_specs=P("section", tokens, None),
        check_vma=False,
    )
```

```python
import jax
import jax.numpy as jnp
from jax import lax
from jax.sharding import Mesh
from jax.sharding import PartitionSpec as P

TOK_BLOCK = 16
QUARTER = ("r", "x")


def passed_along(value, axis, steps):
    count = lax.axis_size(axis)
    pairs = [(source, (source + steps) % count) for source in range(count)]
    return lax.ppermute(value, axis, pairs)


def normalize(inputs, gain_row):
    widened = inputs.astype(jnp.float32)
    mean_sq = jnp.mean(widened * widened, axis=-1, keepdims=True)
    return (widened * lax.rsqrt(mean_sq + 1e-05) * gain_row).astype(jnp.bfloat16)


def route(normed, router_mat, expert_pick, tok_block, capacity):
    logits = jnp.dot(normed, router_mat, preferred_element_type=jnp.float32)
    experts = router_mat.shape[1]
    labels = jnp.arange(experts, dtype=jnp.int32)
    pair_hot = (expert_pick[:, :, None] == labels[None, None, :]).astype(jnp.float32)
    picked = jnp.sum(pair_hot * logits[:, None, :], axis=-1)
    squashed = jax.nn.sigmoid(picked)
    gate_vals = squashed / jnp.sum(squashed, axis=-1, keepdims=True)
    blocks = expert_pick.shape[0] // tok_block
    pair_order = jnp.transpose(expert_pick.reshape(blocks, tok_block, 2), (0, 2, 1)).reshape(
        blocks, 2 * tok_block
    )
    one_hot = (pair_order[:, :, None] == labels[None, None, :]).astype(jnp.int32)
    before = jnp.cumsum(one_hot, axis=1) - one_hot
    pair_ranks = jnp.sum(before * one_hot, axis=-1)
    pair_ranks = jnp.transpose(pair_ranks.reshape(blocks, 2, tok_block), (0, 2, 1)).reshape(-1, 2)
    is_kept = pair_ranks < capacity
    return (gate_vals, pair_ranks, is_kept)


def dispatch(rows, pick, router_mat, capacity, home_q, n_local):
    tok_count, model_width = rows.shape
    tok_block = TOK_BLOCK
    blocks = tok_count // tok_block
    gate_vals, pair_ranks, is_kept = route(rows, router_mat, pick, tok_block, capacity)
    block_of = (jnp.arange(tok_count, dtype=jnp.int32) // tok_block)[:, None]
    here = is_kept & (pick // n_local == home_q)
    slot_ids = (block_of * capacity + pair_ranks) * n_local + pick % n_local
    slot_count = blocks * capacity * n_local
    slot_labels = jnp.arange(slot_count, dtype=jnp.int32)
    slot_hot = ((slot_ids[:, :, None] == slot_labels[None, None, :]) & here[:, :, None]).astype(
        jnp.float32
    )
    placement = jnp.transpose(jnp.sum(slot_hot, axis=1)).astype(jnp.bfloat16)
    combine_mat = jnp.sum(slot_hot * gate_vals[:, :, None], axis=1)
    send_rows = jnp.dot(placement, rows, preferred_element_type=jnp.float32).astype(jnp.bfloat16)
    return send_rows.reshape(blocks * capacity, n_local, model_width), combine_mat


def expert_pass(slot_grid, combine_mat, w_first, w_second):
    lead, n_local, model_width = slot_grid.shape
    n_y = lax.axis_size("y")
    received = lax.all_to_all(slot_grid, QUARTER, split_axis=1, concat_axis=1, tiled=True)
    summed = None
    for k in range(n_y):
        rows_in = received if k == 0 else passed_along(received, "y", k)
        hidden = jax.nn.gelu(
            jnp.dot(rows_in.reshape(-1, model_width), w_first, preferred_element_type=jnp.float32)
        ).astype(jnp.bfloat16)
        partial = jnp.dot(hidden, w_second, preferred_element_type=jnp.float32).astype(jnp.bfloat16)
        if k == 0:
            summed = partial.astype(jnp.float32)
        else:
            summed = summed + passed_along(partial, "y", n_y - k).astype(jnp.float32)
    back = lax.all_to_all(
        summed.astype(jnp.bfloat16).reshape(lead, n_local, model_width),
        QUARTER, split_axis=1, concat_axis=1, tiled=True,
    )
    return jnp.dot(
        combine_mat,
        back.reshape(lead * n_local, model_width).astype(jnp.float32),
        precision=lax.Precision.HIGHEST,
    )


def shifted_pairs(sizes, steps):
    total = 1
    for size in sizes:
        total *= size
    pairs = []
    for source in range(total):
        digits, rest = [], source
        for size in reversed(sizes):
            digits.append(rest % size)
            rest //= size
        digits = digits[::-1]
        dest = 0
        for digit, size, step in zip(digits, sizes, steps):
            dest = dest * size + (digit + step) % size
        pairs.append((source, dest))
    return pairs


def on_device(sent, norm_gain, router, w_in, w_out, expert_ids):
    arrived = passed_along(sent, "section", 1)[0]
    tok_count = arrived.shape[0]
    experts = router.shape[2]
    top_count = expert_ids.shape[2]
    capacity = max(2, (5 * top_count * tok_count + 4 * experts - 1) // (4 * experts))
    n_sec, n_q, n_zh = (lax.axis_size(a) for a in ("section", "q2", "zh"))
    n_local = experts // n_q
    home_q = lax.axis_index("q2")
    offsets = sorted(
        ((a, c) for a in range(n_q) for c in range(n_zh) if (a, c) != (0, 0)),
        key=lambda step: (step[1], -step[0]),
    )
    normed = normalize(arrived, norm_gain[0])
    own_pick = expert_ids[0]
    model_width = normed.shape[1]
    lanes = 128
    tag = jnp.pad(own_pick.astype(jnp.bfloat16), ((0, 0), (0, lanes - top_count)))
    packed = jnp.concatenate([normed, tag], axis=1)
    rows = [normed]
    picks = [own_pick]
    for a, c in offsets:
        far = lax.ppermute(packed, ("q2", "zh"), shifted_pairs((n_q, n_zh), (a, c)))
        rows.append(far[:, :model_width])
        picks.append(far[:, model_width:model_width + top_count].astype(jnp.int32))
    w_first = w_in[0, 0]
    w_second = w_out[0, 0]
    chunk = len(rows) // 2
    halves = []
    for part in (slice(0, chunk), slice(chunk, len(rows))):
        slots, combine = dispatch(
            jnp.concatenate(rows[part], axis=0), jnp.concatenate(picks[part], axis=0),
            router[0], capacity, home_q, n_local,
        )
        halves.append(expert_pass(slots, combine, w_first, w_second))
    sums = jnp.concatenate(halves, axis=0).reshape(len(rows), tok_count, -1)
    steps = [(0, 0)] + offsets
    row_of = [[0] * n_zh for _ in range(n_q)]
    for j, (a, c) in enumerate(steps):
        row_of[a][c] = j
    row_of = jnp.array(row_of, dtype=jnp.int32)
    me_q, me_h = lax.axis_index("q2"), lax.axis_index("zh")
    dest = jnp.arange(n_q * n_zh, dtype=jnp.int32)
    pick_rows = row_of[(me_q - dest // n_zh) % n_q, (me_h - dest % n_zh) % n_zh]
    by_home = jnp.take(sums.astype(jnp.bfloat16), pick_rows, axis=0)
    mine = lax.all_to_all(by_home, ("q2", "zh"), split_axis=0, concat_axis=0, tiled=True)
    combined = arrived.astype(jnp.float32) + jnp.sum(mine.astype(jnp.float32), axis=0)
    return passed_along(combined.astype(jnp.bfloat16)[None], "section", 1)


def solution(mesh):
    sizes = dict(mesh.shape)
    n_expert, n_tensor = sizes["expert"], sizes["tensor"]
    n_x = 4
    fine = Mesh(
        mesh.devices.reshape(sizes["section"], 2, n_expert // (2 * n_x), n_x, n_tensor // 2, 2),
        ("section", "q2", "r", "x", "y", "zh"),
    )
    experts_at = ("q2", "r", "x")
    hidden_units = ("y", "zh")
    tokens = experts_at + hidden_units
    return jax.shard_map(
        on_device,
        mesh=fine,
        in_specs=(
            P("section", tokens, None),
            P("section", None),
            P("section", None, None),
            P("section", experts_at, None, hidden_units),
            P("section", experts_at, hidden_units, None),
            P("section", tokens, None),
        ),
        out_specs=P("section", tokens, None),
        check_vma=False,
    )
```

```python
import jax
import jax.numpy as jnp
from jax import lax
from jax.sharding import Mesh
from jax.sharding import PartitionSpec as P

TOK_BLOCK = 16
QUARTER = ("r", "x")


def passed_along(value, axis, steps):
    count = lax.axis_size(axis)
    pairs = [(source, (source + steps) % count) for source in range(count)]
    return lax.ppermute(value, axis, pairs)


def normalize(inputs, gain_row):
    widened = inputs.astype(jnp.float32)
    mean_sq = jnp.mean(widened * widened, axis=-1, keepdims=True)
    return (widened * lax.rsqrt(mean_sq + 1e-05) * gain_row).astype(jnp.bfloat16)


def route(normed, router_mat, expert_pick, tok_block, capacity):
    logits = jnp.dot(normed, router_mat, preferred_element_type=jnp.float32)
    experts = router_mat.shape[1]
    labels = jnp.arange(experts, dtype=jnp.int32)
    pair_hot = (expert_pick[:, :, None] == labels[None, None, :]).astype(jnp.float32)
    picked = jnp.sum(pair_hot * logits[:, None, :], axis=-1)
    squashed = jax.nn.sigmoid(picked)
    gate_vals = squashed / jnp.sum(squashed, axis=-1, keepdims=True)
    blocks = expert_pick.shape[0] // tok_block
    pair_order = jnp.transpose(expert_pick.reshape(blocks, tok_block, 2), (0, 2, 1)).reshape(
        blocks, 2 * tok_block
    )
    one_hot = (pair_order[:, :, None] == labels[None, None, :]).astype(jnp.int32)
    before = jnp.cumsum(one_hot, axis=1) - one_hot
    pair_ranks = jnp.sum(before * one_hot, axis=-1)
    pair_ranks = jnp.transpose(pair_ranks.reshape(blocks, 2, tok_block), (0, 2, 1)).reshape(-1, 2)
    is_kept = pair_ranks < capacity
    return (gate_vals, pair_ranks, is_kept)


def dispatch(rows, pick, router_mat, capacity, home_q, n_local):
    tok_count, model_width = rows.shape
    tok_block = TOK_BLOCK
    blocks = tok_count // tok_block
    gate_vals, pair_ranks, is_kept = route(rows, router_mat, pick, tok_block, capacity)
    block_of = (jnp.arange(tok_count, dtype=jnp.int32) // tok_block)[:, None]
    here = is_kept & (pick // n_local == home_q)
    slot_ids = (block_of * capacity + pair_ranks) * n_local + pick % n_local
    slot_count = blocks * capacity * n_local
    slot_labels = jnp.arange(slot_count, dtype=jnp.int32)
    slot_hot = ((slot_ids[:, :, None] == slot_labels[None, None, :]) & here[:, :, None]).astype(
        jnp.float32
    )
    placement = jnp.transpose(jnp.sum(slot_hot, axis=1)).astype(jnp.bfloat16)
    combine_mat = jnp.sum(slot_hot * gate_vals[:, :, None], axis=1)
    send_rows = jnp.dot(placement, rows, preferred_element_type=jnp.float32).astype(jnp.bfloat16)
    return send_rows.reshape(blocks * capacity, n_local, model_width), combine_mat


def expert_pass(slot_grid, combine_mat, w_first, w_second):
    lead, n_local, model_width = slot_grid.shape
    n_y = lax.axis_size("y")
    received = lax.all_to_all(slot_grid, QUARTER, split_axis=1, concat_axis=1, tiled=True)
    summed = None
    for k in range(n_y):
        rows_in = received if k == 0 else passed_along(received, "y", k)
        hidden = jax.nn.gelu(
            jnp.dot(rows_in.reshape(-1, model_width), w_first, preferred_element_type=jnp.float32)
        ).astype(jnp.bfloat16)
        partial = jnp.dot(hidden, w_second, preferred_element_type=jnp.float32).astype(jnp.bfloat16)
        if k == 0:
            summed = partial.astype(jnp.float32)
        else:
            summed = summed + passed_along(partial, "y", n_y - k).astype(jnp.float32)
    back = lax.all_to_all(
        summed.astype(jnp.bfloat16).reshape(lead, n_local, model_width),
        QUARTER, split_axis=1, concat_axis=1, tiled=True,
    )
    return jnp.dot(
        combine_mat,
        back.reshape(lead * n_local, model_width).astype(jnp.float32),
        precision=lax.Precision.HIGHEST,
    )


def shifted_pairs(sizes, steps):
    total = 1
    for size in sizes:
        total *= size
    pairs = []
    for source in range(total):
        digits, rest = [], source
        for size in reversed(sizes):
            digits.append(rest % size)
            rest //= size
        digits = digits[::-1]
        dest = 0
        for digit, size, step in zip(digits, sizes, steps):
            dest = dest * size + (digit + step) % size
        pairs.append((source, dest))
    return pairs


def on_device(sent, norm_gain, router, w_in, w_out, expert_ids):
    arrived = passed_along(sent, "section", 1)[0]
    tok_count = arrived.shape[0]
    experts = router.shape[2]
    top_count = expert_ids.shape[2]
    capacity = max(2, (5 * top_count * tok_count + 4 * experts - 1) // (4 * experts))
    n_sec, n_q, n_zh = (lax.axis_size(a) for a in ("section", "q2", "zh"))
    n_local = experts // n_q
    home_q = lax.axis_index("q2")
    offsets = sorted(
        ((a, c) for a in range(n_q) for c in range(n_zh) if (a, c) != (0, 0)),
        key=lambda step: (step[1], -step[0]),
    )
    normed = normalize(arrived, norm_gain[0])
    own_pick = expert_ids[0]
    model_width = normed.shape[1]
    lanes = 128
    tag = jnp.pad(own_pick.astype(jnp.bfloat16), ((0, 0), (0, lanes - top_count)))
    packed = jnp.concatenate([normed, tag], axis=1)
    rows = [normed]
    picks = [own_pick]
    for a, c in offsets:
        far = lax.ppermute(packed, ("q2", "zh"), shifted_pairs((n_q, n_zh), (a, c)))
        rows.append(far[:, :model_width])
        picks.append(far[:, model_width:model_width + top_count].astype(jnp.int32))
    w_first = w_in[0, 0]
    w_second = w_out[0, 0]
    chunk = 1
    halves = []
    for part in (slice(0, chunk), slice(chunk, len(rows))):
        slots, combine = dispatch(
            jnp.concatenate(rows[part], axis=0), jnp.concatenate(picks[part], axis=0),
            router[0], capacity, home_q, n_local,
        )
        halves.append(expert_pass(slots, combine, w_first, w_second))
    sums = jnp.concatenate(halves, axis=0).reshape(len(rows), tok_count, -1)
    combined = arrived.astype(jnp.float32) + sums[0]
    for j, (a, c) in enumerate(offsets, start=1):
        home = shifted_pairs((n_q, n_zh), (-a, -c))
        combined = combined + lax.ppermute(sums[j].astype(jnp.bfloat16), ("q2", "zh"), home).astype(
            jnp.float32
        )
    return passed_along(combined.astype(jnp.bfloat16)[None], "section", 1)


def solution(mesh):
    sizes = dict(mesh.shape)
    n_expert, n_tensor = sizes["expert"], sizes["tensor"]
    n_x = 4
    fine = Mesh(
        mesh.devices.reshape(sizes["section"], 2, n_expert // (2 * n_x), n_x, n_tensor // 2, 2),
        ("section", "q2", "r", "x", "y", "zh"),
    )
    experts_at = ("q2", "r", "x")
    hidden_units = ("y", "zh")
    tokens = experts_at + hidden_units
    return jax.shard_map(
        on_device,
        mesh=fine,
        in_specs=(
            P("section", tokens, None),
            P("section", None),
            P("section", None, None),
            P("section", experts_at, None, hidden_units),
            P("section", experts_at, hidden_units, None),
            P("section", tokens, None),
        ),
        out_specs=P("section", tokens, None),
        check_vma=False,
    )
```

```python
import jax
import jax.numpy as jnp
from jax import lax
from jax.sharding import Mesh
from jax.sharding import PartitionSpec as P

TOK_BLOCK = 16
QUARTER = ("r", "x")


def passed_along(value, axis, steps):
    count = lax.axis_size(axis)
    pairs = [(source, (source + steps) % count) for source in range(count)]
    return lax.ppermute(value, axis, pairs)


def normalize(inputs, gain_row):
    widened = inputs.astype(jnp.float32)
    mean_sq = jnp.mean(widened * widened, axis=-1, keepdims=True)
    return (widened * lax.rsqrt(mean_sq + 1e-05) * gain_row).astype(jnp.bfloat16)


def route(normed, router_mat, expert_pick, tok_block, capacity):
    logits = jnp.dot(normed, router_mat, preferred_element_type=jnp.float32)
    experts = router_mat.shape[1]
    labels = jnp.arange(experts, dtype=jnp.int32)
    pair_hot = (expert_pick[:, :, None] == labels[None, None, :]).astype(jnp.float32)
    picked = jnp.sum(pair_hot * logits[:, None, :], axis=-1)
    squashed = jax.nn.sigmoid(picked)
    gate_vals = squashed / jnp.sum(squashed, axis=-1, keepdims=True)
    blocks = expert_pick.shape[0] // tok_block
    pair_order = jnp.transpose(expert_pick.reshape(blocks, tok_block, 2), (0, 2, 1)).reshape(
        blocks, 2 * tok_block
    )
    one_hot = (pair_order[:, :, None] == labels[None, None, :]).astype(jnp.int32)
    before = jnp.cumsum(one_hot, axis=1) - one_hot
    pair_ranks = jnp.sum(before * one_hot, axis=-1)
    pair_ranks = jnp.transpose(pair_ranks.reshape(blocks, 2, tok_block), (0, 2, 1)).reshape(-1, 2)
    is_kept = pair_ranks < capacity
    return (gate_vals, pair_ranks, is_kept)


def dispatch(rows, pick, router_mat, capacity, home_q, n_local):
    tok_count, model_width = rows.shape
    tok_block = TOK_BLOCK
    blocks = tok_count // tok_block
    gate_vals, pair_ranks, is_kept = route(rows, router_mat, pick, tok_block, capacity)
    block_of = (jnp.arange(tok_count, dtype=jnp.int32) // tok_block)[:, None]
    here = is_kept & (pick // n_local == home_q)
    slot_ids = (block_of * capacity + pair_ranks) * n_local + pick % n_local
    slot_count = blocks * capacity * n_local
    slot_labels = jnp.arange(slot_count, dtype=jnp.int32)
    slot_hot = ((slot_ids[:, :, None] == slot_labels[None, None, :]) & here[:, :, None]).astype(
        jnp.float32
    )
    placement = jnp.transpose(jnp.sum(slot_hot, axis=1)).astype(jnp.bfloat16)
    combine_mat = jnp.sum(slot_hot * gate_vals[:, :, None], axis=1)
    send_rows = jnp.dot(placement, rows, preferred_element_type=jnp.float32).astype(jnp.bfloat16)
    return send_rows.reshape(blocks * capacity, n_local, model_width), combine_mat


def expert_pass(slot_grid, combine_mat, w_first, w_second):
    lead, n_local, model_width = slot_grid.shape
    n_y = lax.axis_size("y")
    received = lax.all_to_all(slot_grid, QUARTER, split_axis=1, concat_axis=1, tiled=True)
    summed = None
    for k in range(n_y):
        rows_in = received if k == 0 else passed_along(received, "y", k)
        hidden = jax.nn.gelu(
            jnp.dot(rows_in.reshape(-1, model_width), w_first, preferred_element_type=jnp.float32)
        ).astype(jnp.bfloat16)
        partial = jnp.dot(hidden, w_second, preferred_element_type=jnp.float32).astype(jnp.bfloat16)
        if k == 0:
            summed = partial.astype(jnp.float32)
        else:
            summed = summed + passed_along(partial, "y", n_y - k).astype(jnp.float32)
    back = lax.all_to_all(
        summed.astype(jnp.bfloat16).reshape(lead, n_local, model_width),
        QUARTER, split_axis=1, concat_axis=1, tiled=True,
    )
    return jnp.dot(
        combine_mat,
        back.reshape(lead * n_local, model_width).astype(jnp.float32),
        precision=lax.Precision.HIGHEST,
    )


def shifted_pairs(sizes, steps):
    total = 1
    for size in sizes:
        total *= size
    pairs = []
    for source in range(total):
        digits, rest = [], source
        for size in reversed(sizes):
            digits.append(rest % size)
            rest //= size
        digits = digits[::-1]
        dest = 0
        for digit, size, step in zip(digits, sizes, steps):
            dest = dest * size + (digit + step) % size
        pairs.append((source, dest))
    return pairs


def layer_body(sent, norm_gain, router, w_in, w_out, expert_ids):
    arrived = passed_along(sent, "section", 1)[0]
    tok_count = arrived.shape[0]
    experts = router.shape[2]
    top_count = expert_ids.shape[2]
    capacity = max(2, (5 * top_count * tok_count + 4 * experts - 1) // (4 * experts))
    _, n_q, n_zh = (lax.axis_size(a) for a in ("section", "q2", "zh"))
    n_local = experts // n_q
    home_q = lax.axis_index("q2")
    offsets = sorted(
        ((a, c) for a in range(n_q) for c in range(n_zh) if (a, c) != (0, 0)),
        key=lambda step: (step[1], -step[0]),
    )
    normed = normalize(arrived, norm_gain[0])
    own_pick = expert_ids[0]
    model_width = normed.shape[1]
    lanes = 128
    tag = jnp.pad(own_pick.astype(jnp.bfloat16), ((0, 0), (0, lanes - top_count)))
    packed = jnp.concatenate([normed, tag], axis=1)
    rows = [normed]
    picks = [own_pick]
    for a, c in offsets:
        far = lax.ppermute(packed, ("q2", "zh"), shifted_pairs((n_q, n_zh), (a, c)))
        rows.append(far[:, :model_width])
        picks.append(far[:, model_width:model_width + top_count].astype(jnp.int32))
    w_first = w_in[0, 0]
    w_second = w_out[0, 0]
    chunk = len(rows) // 2
    halves = []
    for part in (slice(0, chunk), slice(chunk, len(rows))):
        slots, combine = dispatch(
            jnp.concatenate(rows[part], axis=0), jnp.concatenate(picks[part], axis=0),
            router[0], capacity, home_q, n_local,
        )
        halves.append(expert_pass(slots, combine, w_first, w_second))
    sums = jnp.concatenate(halves, axis=0).reshape(len(rows), tok_count, -1)
    combined = arrived.astype(jnp.float32) + sums[0]
    for j, (a, c) in enumerate(offsets, start=1):
        home = shifted_pairs((n_q, n_zh), (-a, -c))
        returned = lax.ppermute(sums[j].astype(jnp.bfloat16), ("q2", "zh"), home)
        combined = combined + returned.astype(jnp.float32)
    return passed_along(combined.astype(jnp.bfloat16)[None], "section", 1)


def solution(mesh):
    sizes = dict(mesh.shape)
    n_expert, n_tensor = sizes["expert"], sizes["tensor"]
    n_x = 4
    fine = Mesh(
        mesh.devices.reshape(sizes["section"], 2, n_expert // (2 * n_x), n_x, n_tensor // 2, 2),
        ("section", "q2", "r", "x", "y", "zh"),
    )
    experts_at = ("q2", "r", "x")
    hidden_units = ("y", "zh")
    tokens = experts_at + hidden_units
    return jax.shard_map(
        layer_body,
        mesh=fine,
        in_specs=(
            P("section", tokens, None),
            P("section", None),
            P("section", None, None),
            P("section", experts_at, None, hidden_units),
            P("section", experts_at, hidden_units, None),
            P("section", tokens, None),
        ),
        out_specs=P("section", tokens, None),
        check_vma=False,
    )
```

```python
import jax
import jax.numpy as jnp
from jax import lax
from jax.sharding import Mesh
from jax.sharding import PartitionSpec as P

TOK_BLOCK = 16
QUARTER = ("r", "x")


def passed_along(value, axis, steps):
    count = lax.axis_size(axis)
    pairs = [(source, (source + steps) % count) for source in range(count)]
    return lax.ppermute(value, axis, pairs)


def normalize(inputs, gain_row):
    widened = inputs.astype(jnp.float32)
    mean_sq = jnp.mean(widened * widened, axis=-1, keepdims=True)
    return (widened * lax.rsqrt(mean_sq + 1e-05) * gain_row).astype(jnp.bfloat16)


def route(normed, router_mat, expert_pick, tok_block, capacity):
    logits = jnp.dot(normed, router_mat, preferred_element_type=jnp.float32)
    experts = router_mat.shape[1]
    labels = jnp.arange(experts, dtype=jnp.int32)
    pair_hot = (expert_pick[:, :, None] == labels[None, None, :]).astype(jnp.float32)
    picked = jnp.sum(pair_hot * logits[:, None, :], axis=-1)
    squashed = jax.nn.sigmoid(picked)
    gate_vals = squashed / jnp.sum(squashed, axis=-1, keepdims=True)
    blocks = expert_pick.shape[0] // tok_block
    pair_order = jnp.transpose(expert_pick.reshape(blocks, tok_block, 2), (0, 2, 1)).reshape(
        blocks, 2 * tok_block
    )
    one_hot = (pair_order[:, :, None] == labels[None, None, :]).astype(jnp.int32)
    before = jnp.cumsum(one_hot, axis=1) - one_hot
    pair_ranks = jnp.sum(before * one_hot, axis=-1)
    pair_ranks = jnp.transpose(pair_ranks.reshape(blocks, 2, tok_block), (0, 2, 1)).reshape(-1, 2)
    is_kept = pair_ranks < capacity
    return (gate_vals, pair_ranks, is_kept)


def dispatch(rows, pick, router_mat, capacity, home_q, n_local):
    tok_count, model_width = rows.shape
    tok_block = TOK_BLOCK
    blocks = tok_count // tok_block
    gate_vals, pair_ranks, is_kept = route(rows, router_mat, pick, tok_block, capacity)
    block_of = (jnp.arange(tok_count, dtype=jnp.int32) // tok_block)[:, None]
    here = is_kept & (pick // n_local == home_q)
    slot_ids = (block_of * capacity + pair_ranks) * n_local + pick % n_local
    slot_count = blocks * capacity * n_local
    slot_labels = jnp.arange(slot_count, dtype=jnp.int32)
    slot_hot = ((slot_ids[:, :, None] == slot_labels[None, None, :]) & here[:, :, None]).astype(
        jnp.float32
    )
    placement = jnp.transpose(jnp.sum(slot_hot, axis=1)).astype(jnp.bfloat16)
    combine_mat = jnp.sum(slot_hot * gate_vals[:, :, None], axis=1)
    send_rows = jnp.dot(placement, rows, preferred_element_type=jnp.float32).astype(jnp.bfloat16)
    return send_rows.reshape(blocks * capacity, n_local, model_width), combine_mat


def expert_pass(slot_grid, combine_mat, w_first, w_second):
    lead, n_local, model_width = slot_grid.shape
    n_y = lax.axis_size("y")
    received = lax.all_to_all(slot_grid, QUARTER, split_axis=1, concat_axis=1, tiled=True)
    far_first = sorted(range(1, n_y), key=lambda k: -min(k, n_y - k))
    arrived_rows = {k: passed_along(received, "y", k) for k in far_first}
    arrived_rows[0] = received
    summed = None
    for k in sorted(range(n_y), key=lambda k: min(k, n_y - k)):
        rows_in = arrived_rows[k]
        hidden = jax.nn.gelu(
            jnp.dot(rows_in.reshape(-1, model_width), w_first, preferred_element_type=jnp.float32)
        ).astype(jnp.bfloat16)
        partial = jnp.dot(hidden, w_second, preferred_element_type=jnp.float32).astype(jnp.bfloat16)
        if k == 0:
            summed = partial.astype(jnp.float32)
        else:
            summed = summed + passed_along(partial, "y", n_y - k).astype(jnp.float32)
    back = lax.all_to_all(
        summed.astype(jnp.bfloat16).reshape(lead, n_local, model_width),
        QUARTER, split_axis=1, concat_axis=1, tiled=True,
    )
    return jnp.dot(
        combine_mat,
        back.reshape(lead * n_local, model_width).astype(jnp.float32),
        precision=lax.Precision.HIGHEST,
    )


def shifted_pairs(sizes, steps):
    total = 1
    for size in sizes:
        total *= size
    pairs = []
    for source in range(total):
        digits, rest = [], source
        for size in reversed(sizes):
            digits.append(rest % size)
            rest //= size
        digits = digits[::-1]
        dest = 0
        for digit, size, step in zip(digits, sizes, steps):
            dest = dest * size + (digit + step) % size
        pairs.append((source, dest))
    return pairs


def on_device(sent, norm_gain, router, w_in, w_out, expert_ids):
    arrived = passed_along(sent, "section", 1)[0]
    tok_count = arrived.shape[0]
    experts = router.shape[2]
    top_count = expert_ids.shape[2]
    capacity = max(2, (5 * top_count * tok_count + 4 * experts - 1) // (4 * experts))
    n_sec, n_q, n_zh = (lax.axis_size(a) for a in ("section", "q2", "zh"))
    n_local = experts // n_q
    home_q = lax.axis_index("q2")
    offsets = sorted(
        ((a, c) for a in range(n_q) for c in range(n_zh) if (a, c) != (0, 0)),
        key=lambda step: (step[1], -step[0]),
    )
    normed = normalize(arrived, norm_gain[0])
    own_pick = expert_ids[0]
    model_width = normed.shape[1]
    lanes = 128
    tag = jnp.pad(own_pick.astype(jnp.bfloat16), ((0, 0), (0, lanes - top_count)))
    packed = jnp.concatenate([normed, tag], axis=1)
    rows = [normed]
    picks = [own_pick]
    for a, c in offsets:
        far = lax.ppermute(packed, ("q2", "zh"), shifted_pairs((n_q, n_zh), (a, c)))
        rows.append(far[:, :model_width])
        picks.append(far[:, model_width:model_width + top_count].astype(jnp.int32))
    w_first = w_in[0, 0]
    w_second = w_out[0, 0]
    chunk = len(rows) // 2
    halves = []
    for part in (slice(0, chunk), slice(chunk, len(rows))):
        slots, combine = dispatch(
            jnp.concatenate(rows[part], axis=0), jnp.concatenate(picks[part], axis=0),
            router[0], capacity, home_q, n_local,
        )
        halves.append(expert_pass(slots, combine, w_first, w_second))
    sums = jnp.concatenate(halves, axis=0).reshape(len(rows), tok_count, -1)
    combined = arrived.astype(jnp.float32) + sums[0]
    for j, (a, c) in enumerate(offsets, start=1):
        home = shifted_pairs((n_q, n_zh), (-a, -c))
        combined = combined + lax.ppermute(sums[j].astype(jnp.bfloat16), ("q2", "zh"), home).astype(
            jnp.float32
        )
    return passed_along(combined.astype(jnp.bfloat16)[None], "section", 1)


def solution(mesh):
    sizes = dict(mesh.shape)
    n_expert, n_tensor = sizes["expert"], sizes["tensor"]
    n_x = 4
    fine = Mesh(
        mesh.devices.reshape(sizes["section"], 2, n_expert // (2 * n_x), n_x, n_tensor // 2, 2),
        ("section", "q2", "r", "x", "y", "zh"),
    )
    experts_at = ("q2", "r", "x")
    hidden_units = ("y", "zh")
    tokens = experts_at + hidden_units
    return jax.shard_map(
        on_device,
        mesh=fine,
        in_specs=(
            P("section", tokens, None),
            P("section", None),
            P("section", None, None),
            P("section", experts_at, None, hidden_units),
            P("section", experts_at, hidden_units, None),
            P("section", tokens, None),
        ),
        out_specs=P("section", tokens, None),
        check_vma=False,
    )
```

```python
import jax
import jax.numpy as jnp
from jax import lax
from jax.sharding import Mesh
from jax.sharding import PartitionSpec as P

TOK_BLOCK = 16
QUARTER = ("r", "x")


def passed_along(value, axis, steps):
    count = lax.axis_size(axis)
    pairs = [(source, (source + steps) % count) for source in range(count)]
    return lax.ppermute(value, axis, pairs)


def normalize(inputs, gain_row):
    widened = inputs.astype(jnp.float32)
    mean_sq = jnp.mean(widened * widened, axis=-1, keepdims=True)
    return (widened * lax.rsqrt(mean_sq + 1e-05) * gain_row).astype(jnp.bfloat16)


def route(normed, router_mat, expert_pick, tok_block, capacity):
    logits = jnp.dot(normed, router_mat, preferred_element_type=jnp.float32)
    experts = router_mat.shape[1]
    labels = jnp.arange(experts, dtype=jnp.int32)
    pair_hot = (expert_pick[:, :, None] == labels[None, None, :]).astype(jnp.float32)
    picked = jnp.sum(pair_hot * logits[:, None, :], axis=-1)
    squashed = jax.nn.sigmoid(picked)
    gate_vals = squashed / jnp.sum(squashed, axis=-1, keepdims=True)
    blocks = expert_pick.shape[0] // tok_block
    pair_order = jnp.transpose(expert_pick.reshape(blocks, tok_block, 2), (0, 2, 1)).reshape(
        blocks, 2 * tok_block
    )
    one_hot = (pair_order[:, :, None] == labels[None, None, :]).astype(jnp.int32)
    before = jnp.cumsum(one_hot, axis=1) - one_hot
    pair_ranks = jnp.sum(before * one_hot, axis=-1)
    pair_ranks = jnp.transpose(pair_ranks.reshape(blocks, 2, tok_block), (0, 2, 1)).reshape(-1, 2)
    is_kept = pair_ranks < capacity
    return (gate_vals, pair_ranks, is_kept)


def dispatch(rows, pick, router_mat, capacity, home_q, n_local):
    tok_count, model_width = rows.shape
    tok_block = TOK_BLOCK
    blocks = tok_count // tok_block
    gate_vals, pair_ranks, is_kept = route(rows, router_mat, pick, tok_block, capacity)
    block_of = (jnp.arange(tok_count, dtype=jnp.int32) // tok_block)[:, None]
    here = is_kept & (pick // n_local == home_q)
    slot_ids = (block_of * capacity + pair_ranks) * n_local + pick % n_local
    slot_count = blocks * capacity * n_local
    slot_labels = jnp.arange(slot_count, dtype=jnp.int32)
    slot_hot = ((slot_ids[:, :, None] == slot_labels[None, None, :]) & here[:, :, None]).astype(
        jnp.float32
    )
    placement = jnp.transpose(jnp.sum(slot_hot, axis=1)).astype(jnp.bfloat16)
    combine_mat = jnp.sum(slot_hot * gate_vals[:, :, None], axis=1)
    send_rows = jnp.dot(placement, rows, preferred_element_type=jnp.float32).astype(jnp.bfloat16)
    return send_rows.reshape(blocks * capacity, n_local, model_width), combine_mat


def expert_pass(slot_grid, combine_mat, w_first, w_second):
    lead, n_local, model_width = slot_grid.shape
    n_y = lax.axis_size("y")
    received = lax.all_to_all(slot_grid, QUARTER, split_axis=1, concat_axis=1, tiled=True)
    far_first = sorted(range(1, n_y), key=lambda k: -min(k, n_y - k))
    arrived_rows = {k: passed_along(received, "y", k) for k in far_first}
    arrived_rows[0] = received
    summed = None
    for k in sorted(range(n_y), key=lambda k: min(k, n_y - k)):
        rows_in = arrived_rows[k]
        hidden = jax.nn.gelu(
            jnp.dot(rows_in.reshape(-1, model_width), w_first, preferred_element_type=jnp.float32)
        ).astype(jnp.bfloat16)
        partial = jnp.dot(hidden, w_second, preferred_element_type=jnp.float32).astype(jnp.bfloat16)
        if k == 0:
            summed = partial.astype(jnp.float32)
        else:
            summed = summed + passed_along(partial, "y", n_y - k).astype(jnp.float32)
    back = lax.all_to_all(
        summed.astype(jnp.bfloat16).reshape(lead, n_local, model_width),
        QUARTER, split_axis=1, concat_axis=1, tiled=True,
    )
    return jnp.dot(
        combine_mat,
        back.reshape(lead * n_local, model_width).astype(jnp.float32),
        precision=lax.Precision.HIGHEST,
    )


def shifted_pairs(sizes, steps):
    total = 1
    for size in sizes:
        total *= size
    pairs = []
    for source in range(total):
        digits, rest = [], source
        for size in reversed(sizes):
            digits.append(rest % size)
            rest //= size
        digits = digits[::-1]
        dest = 0
        for digit, size, step in zip(digits, sizes, steps):
            dest = dest * size + (digit + step) % size
        pairs.append((source, dest))
    return pairs


def on_device(sent, norm_gain, router, w_in, w_out, expert_ids):
    arrived = passed_along(sent, "section", 1)[0]
    tok_count = arrived.shape[0]
    experts = router.shape[2]
    top_count = expert_ids.shape[2]
    capacity = max(2, (5 * top_count * tok_count + 4 * experts - 1) // (4 * experts))
    n_sec, n_q, n_zh = (lax.axis_size(a) for a in ("section", "q2", "zh"))
    n_local = experts // n_q
    home_q = lax.axis_index("q2")
    offsets = sorted(
        ((a, c) for a in range(n_q) for c in range(n_zh) if (a, c) != (0, 0)),
        key=lambda step: (step[1], -step[0]),
    )
    normed = normalize(arrived, norm_gain[0])
    own_pick = expert_ids[0]
    model_width = normed.shape[1]
    lanes = 128
    tag = jnp.pad(own_pick.astype(jnp.bfloat16), ((0, 0), (0, lanes - top_count)))
    packed = jnp.concatenate([normed, tag], axis=1)
    rows = [normed]
    picks = [own_pick]
    for a, c in offsets:
        far = lax.ppermute(packed, ("q2", "zh"), shifted_pairs((n_q, n_zh), (a, c)))
        rows.append(far[:, :model_width])
        picks.append(far[:, model_width:model_width + top_count].astype(jnp.int32))
    w_first = w_in[0, 0]
    w_second = w_out[0, 0]
    chunk = len(rows) // 2
    halves = []
    for part in (slice(0, chunk), slice(chunk, len(rows))):
        slots, combine = dispatch(
            jnp.concatenate(rows[part], axis=0), jnp.concatenate(picks[part], axis=0),
            router[0], capacity, home_q, n_local,
        )
        halves.append(expert_pass(slots, combine, w_first, w_second))
    sums = jnp.concatenate(halves, axis=0).reshape(len(rows), tok_count, -1)
    combined = arrived.astype(jnp.float32) + sums[0]
    for j, (a, c) in sorted(enumerate(offsets, start=1), key=lambda item: -item[1][1]):
        home = shifted_pairs((n_q, n_zh), (-a, -c))
        combined = combined + lax.ppermute(sums[j].astype(jnp.bfloat16), ("q2", "zh"), home).astype(
            jnp.float32
        )
    return passed_along(combined.astype(jnp.bfloat16)[None], "section", 1)


def solution(mesh):
    sizes = dict(mesh.shape)
    n_expert, n_tensor = sizes["expert"], sizes["tensor"]
    n_x = 4
    fine = Mesh(
        mesh.devices.reshape(sizes["section"], 2, n_expert // (2 * n_x), n_x, n_tensor // 2, 2),
        ("section", "q2", "r", "x", "y", "zh"),
    )
    experts_at = ("q2", "r", "x")
    hidden_units = ("y", "zh")
    tokens = experts_at + hidden_units
    return jax.shard_map(
        on_device,
        mesh=fine,
        in_specs=(
            P("section", tokens, None),
            P("section", None),
            P("section", None, None),
            P("section", experts_at, None, hidden_units),
            P("section", experts_at, hidden_units, None),
            P("section", tokens, None),
        ),
        out_specs=P("section", tokens, None),
        check_vma=False,
    )
```
